256 devices in a mesh: fsdp: 16 (over z, core), batch: 16 (over y, x).
Axes of the slice: x: 4, y: 4, z: 8, core: 2. Of those that a mesh axis runs over, the one named last changes fastest.
Arguments:
- latents: bfloat16 [16, 16, 1024, 640], P('batch', 'fsdp'), may hold values from -6 to 6
- norm_gain: float32 [640], replicated, may hold values from 0.25 to 1.75
- second_gain: float32 [640], replicated, may hold values from 0.25 to 1.75
- spatial_w: bfloat16 [9, 640, 640], P(None, None, 'fsdp'), may hold values from -0.078125 to 0.078125
- temporal_w: bfloat16 [3, 640, 640], P(None, None, 'fsdp'), may hold values from -0.125 to 0.125
- critic_w: bfloat16 [16, 640, 640], P('batch'), may hold values from -0.25 to 0.25
- critic_head: float32 [16, 640], P('batch'), may hold values from -6 to 6
- targets: int32 [16, 32, 1], P('batch'), may hold values from 0 to 15; in each aligned block of 32 rows (0 to 31, 32 to 63, ..., all dimensions but the last counted through in order) at most 4 rows name the same one
- feasible: int32 [16, 16], P('batch', 'fsdp'), may hold values 0 or 1
Outputs:
- guided: bfloat16 [16, 16, 1024, 640], P('batch', 'fsdp')
The draws below stay inside these ranges and needn't reach their ends.
Inputs may be any that keep to these rules, and one draw needn't show every extreme that they name: `targets`: among one candidate's 32 rows no critic group is named more than 4 times.
All inputs are finite; a program needn't handle non-finite values. No bound on the sum of `feasible` on one device may be relied on, other than what follows from the above.
Results may differ from the reference program's by a relative error of at most 0.0065.
Values may be sent and summed in bfloat16 or wider, within the bound.
No kernel may reach another device: no remote copies, remote signals or barrier semaphores. Data moves between devices by JAX's collectives and lax.ppermute only.
A program may use at most 128 MiB of HBM per device.

```python
import math
import jax
import jax.numpy as jnp
import numpy as np
from jax import lax

C = 640
HID = 640
GROUPS = 32
IMG_ROWS = 32
IMG_COLS = 32
PIX = 1024
FRAMES = 16
CANDIDATES = 16
CAP = 4
N_BATCH = 16


def touch_ends(entries, stream_key, least, largest):
    longest = entries.shape.index(max(entries.shape))
    spots = []
    for shift in (0, 1):
        where = [jax.random.randint(jax.random.fold_in(stream_key, axis), (), 0, length) for axis, length in enumerate(entries.shape)]
        where[longest] = (where[longest] + shift) % entries.shape[longest]
        spots.append(tuple(where))
    return entries.at[spots[0]].set(least).at[spots[1]].set(largest)


def block_levels(key, shape, split, smallest, top_value):
    level, own = 1.0, jax.random.fold_in(key, 6)
    for position, blocks in split:
        steps = jnp.exp(jax.random.uniform(jax.random.fold_in(own, position), (blocks,), jnp.float32, smallest / len(split), top_value / len(split)))
        level = level * jnp.repeat(steps, shape[position] // blocks).reshape([-1 if axis == position else 1 for axis in range(len(shape))])
    return level


def assign_block(rng, own, number, rows, count, top, reach, skew):
    order = jax.random.permutation(rng, count)
    heavy_load, common = load_shares(count, rows * top, reach, skew, True), load_shares(count, rows * top, reach, skew, False)
    places = jnp.arange(count)

    def named(lengths, rotation):
        used = int((lengths > 0).sum())
        fixed = max(1, used // 4)
        shifted = fixed + (places - fixed + rotation * (used - fixed)) % max(1, count - fixed)
        return jnp.zeros((count,), jnp.int32).at[order[jnp.where(places < fixed, places, shifted)]].set(jnp.asarray(lengths, jnp.int32))

    lengths = jnp.where(number % 4 == 0, named(heavy_load, number // 4), named(common, number - number // 4 - 1))
    mixed = jax.random.permutation(jax.random.fold_in(own, 3), count)
    giver, sink = mixed[0:count // 2 * 2:2], mixed[1:count // 2 * 2:2]
    room = jnp.minimum(lengths[giver] - 1, reach - lengths[sink]) // 2
    room = jnp.where((giver == order[0]) | (sink == order[0]) | (lengths[sink] == 0), 0, jnp.maximum(room, 0))
    shifted = jax.random.randint(jax.random.fold_in(own, 4), (count // 2,), 0, 1 << 20) % (room + 1)
    lengths = lengths.at[giver].add(-shifted).at[sink].add(shifted)
    members = jnp.searchsorted(jnp.cumsum(lengths), jnp.arange(rows * top), side="right").astype(jnp.int32)
    listing = members.reshape(top, rows).T
    listing = listing[jax.random.permutation(jax.random.fold_in(own, 1), rows)]
    rotation = jax.random.randint(jax.random.fold_in(own, 2), (rows, 1), 0, top)
    return jnp.take_along_axis(listing, (jnp.arange(top)[None, :] + rotation) % top, axis=1)


def load_shares(number_of, total, bound, skew, full):
    loads = [(1 << 20) // math.isqrt(grade ** skew) + 1 for grade in range(1, number_of + 1)]
    largest = bound if full else min(bound, max(-(-total // number_of), total * loads[0] // sum(loads)))
    least = 1 if total - largest >= number_of - 1 else 0
    given, rest = [largest] + [least] * (number_of - 1), total - largest - least * (number_of - 1)
    while rest > 0:
        free = [i for i in range(1, number_of) if given[i] < largest] or [i for i in range(1, number_of) if given[i] < bound]
        whole, budget = sum([loads[i] for i in free]), rest
        for i in free:
            extra = min(bound - given[i], max(1, budget * loads[i] // whole), rest)
            given[i] = given[i] + extra
            rest = rest - extra
    return np.array(given)


def scatter_about(rng, shape, scale, bound, pieces=(), dtype=jnp.bfloat16):
    array = scale * jax.random.normal(rng, shape, jnp.float32)
    if pieces:
        array = array * block_levels(rng, shape, pieces, -0.22, 0.18)
    return jnp.clip(array, -bound, bound).astype(dtype)


def setup_inputs(seed: int = 0) -> dict:
    key_of = jax.random.split(jax.random.key(seed), 10)
    latents = scatter_about(key_of[0], (CANDIDATES, FRAMES, PIX, C), 1.0, 6.0, ((0, 16), (1, 16)))
    norm_gain = jnp.clip(1.0 + 0.15 * jax.random.normal(key_of[1], (C,), jnp.float32), 0.25, 1.75)
    second_gain = jnp.clip(1.0 + 0.15 * jax.random.normal(key_of[2], (C,), jnp.float32), 0.25, 1.75)
    spatial_w = scatter_about(key_of[3], (9, C, C), (9 * C) ** -0.5, 0.078125, ((2, 16),))
    temporal_w = scatter_about(key_of[4], (3, C, C), (3 * C) ** -0.5, 0.125, ((2, 16),))
    critic_w = scatter_about(key_of[5], (N_BATCH, C, HID), C ** -0.5, 0.25, ((0, 16),))
    critic_head = scatter_about(key_of[6], (N_BATCH, HID), 1.0, 6.0, ((0, 16),), jnp.float32)
    targets_keys = jax.random.split(jax.random.fold_in(key_of[7], 1), CANDIDATES * IMG_ROWS // IMG_ROWS)
    targets_turns = jax.random.permutation(jax.random.fold_in(key_of[7], 3), CANDIDATES * IMG_ROWS // IMG_ROWS)
    targets = jax.vmap(lambda own, number: assign_block(jax.random.fold_in(key_of[7], 2), own, number, IMG_ROWS, N_BATCH, 1, CAP, 1))(targets_keys, targets_turns).reshape((CANDIDATES, IMG_ROWS, 1))
    feasible = touch_ends((jax.random.randint(key_of[8], (CANDIDATES, FRAMES), 0, 4) < 3).astype(jnp.int32), jax.random.fold_in(key_of[8], 1), 0, 1)
    return dict(latents=latents, norm_gain=norm_gain, second_gain=second_gain, spatial_w=spatial_w, temporal_w=temporal_w, critic_w=critic_w, critic_head=critic_head, targets=targets, feasible=feasible)


def group_silu(values, gain):
    shape = values.shape
    width = shape[-1]
    grouped = values.astype(jnp.float32).reshape(shape[0], shape[1], GROUPS, width // GROUPS)
    center = lax.optimization_barrier(jnp.mean(grouped, axis=(1, 3), keepdims=True))
    spread = lax.optimization_barrier(jnp.mean((grouped - center) ** 2, axis=(1, 3), keepdims=True))
    normed = ((grouped - center) * lax.rsqrt(spread + 1e-05)).reshape(shape) * gain
    return jax.nn.silu(normed).astype(jnp.bfloat16)

def one_plan(latent, target_rows, listed, norm_gain, second_gain, spatial_w, temporal_w, critic_w, critic_head):
    frames_all = latent.shape[0]
    width = latent.shape[-1]
    first = group_silu(latent, norm_gain)
    padded = jnp.pad(first.reshape(frames_all, IMG_ROWS, IMG_COLS, width), ((0, 0), (1, 1), (1, 1), (0, 0)))
    mixed = jnp.zeros((frames_all * PIX, width), jnp.float32)
    for offset in range(9):
        row_off, col_off = divmod(offset, 3)
        window = padded[:, row_off:row_off + IMG_ROWS, col_off:col_off + IMG_COLS].reshape(-1, width)
        mixed = mixed + jnp.dot(window, spatial_w[offset], preferred_element_type=jnp.float32)
    section = (latent.astype(jnp.float32) + mixed.reshape(latent.shape)).astype(jnp.bfloat16)
    second = group_silu(section, second_gain)
    framed = jnp.pad(second, ((1, 1), (0, 0), (0, 0)))
    motion = jnp.zeros((frames_all * PIX, width), jnp.float32)
    for tap in range(3):
        motion = motion + jnp.dot(framed[tap:tap + frames_all].reshape(-1, width), temporal_w[tap], preferred_element_type=jnp.float32)
    denoised = (section.astype(jnp.float32) + motion.reshape(latent.shape)).astype(jnp.bfloat16)
    chosen = target_rows[:, 0]
    picked = critic_w[chosen].astype(jnp.float32)
    heads = critic_head[chosen]
    rowwise = denoised.reshape(frames_all, IMG_ROWS, IMG_COLS, width).astype(jnp.float32)
    pre = jnp.einsum('frpc,rch->frph', rowwise, picked)
    slope = ((1.0 - jnp.tanh(pre) ** 2) * heads[None, :, None, :]).astype(jnp.bfloat16)
    grad = jnp.einsum('frph,rch->frpc', slope.astype(jnp.float32), picked).astype(jnp.bfloat16)
    scale = listed.astype(jnp.float32)[:, None, None]
    return (denoised.astype(jnp.float32) - scale * grad.astype(jnp.float32).reshape(latent.shape)).astype(jnp.bfloat16)

def reference(latents, norm_gain, second_gain, spatial_w, temporal_w, critic_w, critic_head, targets, feasible):

    def step_one(items):
        latent, target_rows, listed = items
        return one_plan(latent, target_rows, listed, norm_gain, second_gain, spatial_w, temporal_w, critic_w, critic_head)
    return lax.map(step_one, (latents, targets, feasible))
```

```python
import jax
import jax.numpy as jnp
from jax import lax
from jax.sharding import PartitionSpec as P

GROUPS = 32
IMG_ROWS = 32
IMG_COLS = 32
PIX = 1024
CAP = 4


def with_halo(array, sides, width):
    for axis, dim in sides:
        size, length = (lax.axis_size(axis), array.shape[dim])
        up = [(i, (i + 1) % size) for i in range(size - 1)]
        down = [(j, i) for i, j in up]
        last = lax.slice_in_dim(array, length - width, length, axis=dim)
        leading = lax.slice_in_dim(array, 0, width, axis=dim)
        before = lax.ppermute(last, axis, up)
        after = lax.ppermute(leading, axis, down)
        array = jnp.concatenate([before, array, after], axis=dim)
    return array


def group_silu(values, gain):
    shape = values.shape
    width = shape[-1]
    grouped = values.astype(jnp.float32).reshape(-1, shape[-2], GROUPS, width // GROUPS)
    center = jnp.mean(grouped, axis=(1, 3), keepdims=True)
    spread = jnp.mean((grouped - center) ** 2, axis=(1, 3), keepdims=True)
    normed = ((grouped - center) * lax.rsqrt(spread + 1e-05)).reshape(shape) * gain
    return jax.nn.silu(normed).astype(jnp.bfloat16)


def per_device(
    latents, norm_gain, second_gain, spatial_w, temporal_w, critic_w, critic_head, targets, feasible
):
    cands = latents.shape[0]
    width = latents.shape[-1]
    first = group_silu(latents, norm_gain)
    padded = jnp.pad(
        first.reshape(cands, IMG_ROWS, IMG_COLS, width), ((0, 0), (1, 1), (1, 1), (0, 0))
    )
    spatial_full = lax.all_gather(spatial_w, "fsdp", axis=2, tiled=True)
    temporal_full = lax.all_gather(temporal_w, "fsdp", axis=2, tiled=True)
    total = jnp.zeros((cands * PIX, spatial_full.shape[2]), jnp.float32)
    for offset in range(9):
        row_off, col_off = divmod(offset, 3)
        window = padded[:, row_off : row_off + IMG_ROWS, col_off : col_off + IMG_COLS].reshape(
            -1, width
        )
        total = total + jnp.dot(window, spatial_full[offset], preferred_element_type=jnp.float32)
    section = (latents.astype(jnp.float32) + total.reshape(latents.shape)).astype(jnp.bfloat16)
    second = group_silu(section, second_gain)
    beside_all = with_halo(second, (("fsdp", 1),), 1)
    total = jnp.zeros((cands * PIX, temporal_full.shape[2]), jnp.float32)
    for tap in range(3):
        total = total + jnp.dot(
            beside_all[:, tap].reshape(-1, width),
            temporal_full[tap],
            preferred_element_type=jnp.float32,
        )
    denoised = (section.astype(jnp.float32) + total.reshape(latents.shape)).astype(jnp.bfloat16)

    groups = lax.axis_size("batch")
    slots = cands * CAP
    flat_targets = targets.reshape(-1)
    chosen = (flat_targets[:, None] == jnp.arange(groups, dtype=jnp.int32)[None, :]).astype(
        jnp.int32
    )
    earlier = jnp.cumsum(chosen, axis=0) - chosen
    slot_of = jnp.sum(earlier * chosen, axis=1)
    live = jnp.repeat(feasible.reshape(-1), IMG_ROWS) > 0
    position = flat_targets * slots + slot_of
    placing = (
        (jnp.arange(groups * slots, dtype=jnp.int32)[:, None] == position[None, :]) & live[None, :]
    ).astype(jnp.bfloat16)
    rows = denoised.reshape(cands * IMG_ROWS, IMG_COLS * width)
    outgoing = (
        jnp.dot(placing, rows, preferred_element_type=jnp.float32)
        .astype(jnp.bfloat16)
        .reshape(groups, slots * IMG_COLS, width)
    )
    arrived = lax.all_to_all(outgoing, "batch", 0, 0, tiled=True)
    own_w = critic_w[0]
    pre = jnp.dot(arrived.reshape(-1, width), own_w, preferred_element_type=jnp.float32)
    slope = ((1.0 - jnp.tanh(pre) ** 2) * critic_head[0][None, :]).astype(jnp.bfloat16)
    grads = lax.dot_general(
        slope, own_w, (((1,), (1,)), ((), ())), preferred_element_type=jnp.float32
    ).astype(jnp.bfloat16)
    returned = lax.all_to_all(
        grads.reshape(groups, slots * IMG_COLS, width), "batch", 0, 0, tiled=True
    )
    back = jnp.dot(
        placing.T, returned.reshape(groups * slots, -1), preferred_element_type=jnp.float32
    )
    guided = (rows.astype(jnp.float32) - back).astype(jnp.bfloat16)
    return guided.reshape(latents.shape)


def solution(mesh):
    in_specs = (
        P("batch", "fsdp", None, None),
        P(),
        P(),
        P(None, None, "fsdp"),
        P(None, None, "fsdp"),
        P("batch", None, None),
        P("batch", None),
        P("batch", None, None),
        P("batch", "fsdp"),
    )
    out_specs = P("batch", "fsdp", None, None)
    return jax.shard_map(
        per_device, mesh=mesh, in_specs=in_specs, out_specs=out_specs, check_vma=False
    )
```

```python
import jax
import jax.numpy as jnp
import numpy as np
from jax import lax
from jax.sharding import Mesh
from jax.sharding import PartitionSpec as P

GROUPS = 32
IMG_ROWS = 32
IMG_COLS = 32
PIX = 1024
CAP = 4
FSDP = ("z", "c")
BATCH = ("y", "x")


def with_halo(array, axis, dim):
    size, length = (lax.axis_size(axis), array.shape[dim])
    up = [(i, (i + 1) % size) for i in range(size - 1)]
    down = [(j, i) for i, j in up]
    last = lax.slice_in_dim(array, length - 1, length, axis=dim)
    leading = lax.slice_in_dim(array, 0, 1, axis=dim)
    before = lax.ppermute(last, axis, up)
    after = lax.ppermute(leading, axis, down)
    return jnp.concatenate([before, array, after], axis=dim)


def group_silu(values, gain):
    shape = values.shape
    width = shape[-1]
    grouped = values.astype(jnp.float32).reshape(-1, shape[-2], GROUPS, width // GROUPS)
    center = jnp.mean(grouped, axis=(1, 3), keepdims=True)
    spread = jnp.mean((grouped - center) ** 2, axis=(1, 3), keepdims=True)
    normed = ((grouped - center) * lax.rsqrt(spread + 1e-05)).reshape(shape) * gain
    return jax.nn.silu(normed).astype(jnp.bfloat16)


def gather_out_major(weights):
    turned = jnp.swapaxes(weights, 1, 2)
    return lax.all_gather(turned, FSDP, axis=1, tiled=True)


def nt_dot(a, b):
    return lax.dot_general(a, b, (((1,), (1,)), ((), ())), preferred_element_type=jnp.float32)


def per_device(
    latents, norm_gain, second_gain, spatial_w, temporal_w, critic_w, critic_head, targets, feasible
):
    cands = latents.shape[0]
    width = latents.shape[-1]
    hid = critic_w.shape[-1]

    core = lax.axis_index("c")
    half = hid // 2
    own_half = lax.dynamic_slice_in_dim(critic_w[0], core * half, half, axis=1)
    mine = lax.all_gather(own_half, BATCH, axis=0, tiled=False)
    other = lax.ppermute(mine, "c", [(0, 1), (1, 0)])
    heads = lax.all_gather(critic_head[0], BATCH, axis=0, tiled=False)
    heads_mine = lax.dynamic_slice_in_dim(heads, core * half, half, axis=1)
    heads_other = lax.dynamic_slice_in_dim(heads, (1 - core) * half, half, axis=1)

    spatial_full = gather_out_major(spatial_w)
    temporal_full = gather_out_major(temporal_w)

    first = group_silu(latents, norm_gain)
    padded = jnp.pad(
        first.reshape(cands, IMG_ROWS, IMG_COLS, width), ((0, 0), (1, 1), (1, 1), (0, 0))
    )
    total = jnp.zeros((cands * PIX, spatial_full.shape[1]), jnp.float32)
    for offset in range(9):
        row_off, col_off = divmod(offset, 3)
        window = padded[:, row_off : row_off + IMG_ROWS, col_off : col_off + IMG_COLS].reshape(
            -1, width
        )
        total = total + nt_dot(window, spatial_full[offset])
    section = (latents.astype(jnp.float32) + total.reshape(latents.shape)).astype(jnp.bfloat16)
    second = group_silu(section, second_gain)
    beside_all = with_halo(second, FSDP, 1)
    total = jnp.zeros((cands * PIX, temporal_full.shape[1]), jnp.float32)
    for tap in range(3):
        total = total + nt_dot(beside_all[:, tap].reshape(-1, width), temporal_full[tap])
    denoised = (section.astype(jnp.float32) + total.reshape(latents.shape)).astype(jnp.bfloat16)

    groups = mine.shape[0]
    slots = cands * CAP
    flat_targets = targets.reshape(-1)
    chosen = (flat_targets[:, None] == jnp.arange(groups, dtype=jnp.int32)[None, :]).astype(
        jnp.int32
    )
    earlier = jnp.cumsum(chosen, axis=0) - chosen
    slot_of = jnp.sum(earlier * chosen, axis=1)
    live = jnp.repeat(feasible.reshape(-1), IMG_ROWS) > 0
    position = flat_targets * slots + slot_of
    placing = (
        (jnp.arange(groups * slots, dtype=jnp.int32)[:, None] == position[None, :]) & live[None, :]
    ).astype(jnp.bfloat16)
    rows = denoised.reshape(cands * IMG_ROWS, IMG_COLS * width)
    block = (
        jnp.dot(placing, rows, preferred_element_type=jnp.float32)
        .astype(jnp.bfloat16)
        .reshape(groups, slots * IMG_COLS, width)
    )

    def slope_of(w, h):
        pre = jnp.einsum("gtc,gch->gth", block, w, preferred_element_type=jnp.float32)
        return ((1.0 - jnp.tanh(pre) ** 2) * h[:, None, :]).astype(jnp.bfloat16)

    grads = jnp.einsum(
        "gth,gch->gtc", slope_of(mine, heads_mine), mine, preferred_element_type=jnp.float32
    ) + jnp.einsum(
        "gth,gch->gtc", slope_of(other, heads_other), other, preferred_element_type=jnp.float32
    )
    returned = grads.astype(jnp.bfloat16).reshape(groups * slots, -1)
    back = jnp.dot(placing.T, returned, preferred_element_type=jnp.float32)
    guided = (rows.astype(jnp.float32) - back).astype(jnp.bfloat16)
    return guided.reshape(latents.shape)


def solution(mesh):
    fine = Mesh(np.asarray(mesh.devices).reshape(8, 2, 4, 4), ("z", "c", "y", "x"))
    in_specs = (
        P(BATCH, FSDP, None, None),
        P(),
        P(),
        P(None, None, FSDP),
        P(None, None, FSDP),
        P(BATCH, None, None),
        P(BATCH, None),
        P(BATCH, None, None),
        P(BATCH, FSDP),
    )
    out_specs = P(BATCH, FSDP, None, None)
    return jax.shard_map(
        per_device, mesh=fine, in_specs=in_specs, out_specs=out_specs, check_vma=False
    )
```

```python
import jax
import jax.numpy as jnp
import numpy as np
from jax import lax
from jax.sharding import Mesh
from jax.sharding import PartitionSpec as P

GROUPS = 32
IMG_ROWS = 32
IMG_COLS = 32
PIX = 1024
CAP = 4
FSDP = ("z", "c")
BATCH = ("y", "x")


def with_halo(array, axis, dim):
    size, length = (lax.axis_size(axis), array.shape[dim])
    up = [(i, (i + 1) % size) for i in range(size - 1)]
    down = [(j, i) for i, j in up]
    last = lax.slice_in_dim(array, length - 1, length, axis=dim)
    leading = lax.slice_in_dim(array, 0, 1, axis=dim)
    before = lax.ppermute(last, axis, up)
    after = lax.ppermute(leading, axis, down)
    return jnp.concatenate([before, array, after], axis=dim)


def group_silu(values, gain):
    shape = values.shape
    width = shape[-1]
    grouped = values.astype(jnp.float32).reshape(-1, shape[-2], GROUPS, width // GROUPS)
    center = jnp.mean(grouped, axis=(1, 3), keepdims=True)
    spread = jnp.mean((grouped - center) ** 2, axis=(1, 3), keepdims=True)
    normed = ((grouped - center) * lax.rsqrt(spread + 1e-05)).reshape(shape) * gain
    return jax.nn.silu(normed).astype(jnp.bfloat16)


def gather_out_major(weights):
    turned = jnp.swapaxes(weights, 1, 2)
    return lax.all_gather(turned, FSDP, axis=1, tiled=True)


def ring_gather(parts, axis):
    size = lax.axis_size(axis)
    fwd = [(i, (i + 1) % size) for i in range(size)]
    bwd = [(i, (i - 1) % size) for i in range(size)]
    out = []
    for v in parts:
        from_m1 = lax.ppermute(v, axis, fwd)
        from_p1 = lax.ppermute(v, axis, bwd)
        cut = v.shape[-1] // 2
        left = lax.ppermute(from_m1[..., :cut], axis, fwd)
        right = lax.ppermute(from_p1[..., cut:], axis, bwd)
        from_m2 = jnp.concatenate([left, right], axis=-1)
        out.append(jnp.stack([from_m2, from_m1, v, from_p1]))
    return tuple(out)


def nt_dot(a, b):
    return lax.dot_general(a, b, (((1,), (1,)), ((), ())), preferred_element_type=jnp.float32)


def per_device(
    latents, norm_gain, second_gain, spatial_w, temporal_w, critic_w, critic_head, targets, feasible
):
    cands = latents.shape[0]
    width = latents.shape[-1]
    hid = critic_w.shape[-1]

    core = lax.axis_index("c")
    half = hid // 2
    own = (
        lax.dynamic_slice_in_dim(critic_w[0], core * half, half, axis=1),
        lax.dynamic_slice_in_dim(critic_head[0], core * half, half, axis=0),
    )
    along_x = ring_gather(own, "x")
    mine = ring_gather(along_x, "y")
    mine = tuple(m.reshape(-1, *m.shape[2:]) for m in mine)
    other = tuple(lax.ppermute(m, "c", [(0, 1), (1, 0)]) for m in mine)

    joint = jnp.concatenate([spatial_w, temporal_w], axis=0)
    joint_full = gather_out_major(joint)
    spatial_full = joint_full[: spatial_w.shape[0]]
    temporal_full = joint_full[spatial_w.shape[0] :]

    first = group_silu(latents, norm_gain)
    padded = jnp.pad(
        first.reshape(cands, IMG_ROWS, IMG_COLS, width), ((0, 0), (1, 1), (1, 1), (0, 0))
    )
    total = jnp.zeros((cands * PIX, spatial_full.shape[1]), jnp.float32)
    for offset in range(9):
        row_off, col_off = divmod(offset, 3)
        window = padded[:, row_off : row_off + IMG_ROWS, col_off : col_off + IMG_COLS].reshape(
            -1, width
        )
        total = total + nt_dot(window, spatial_full[offset])
    section = (latents.astype(jnp.float32) + total.reshape(latents.shape)).astype(jnp.bfloat16)
    second = group_silu(section, second_gain)
    beside_all = with_halo(second, FSDP, 1)
    total = jnp.zeros((cands * PIX, temporal_full.shape[1]), jnp.float32)
    for tap in range(3):
        total = total + nt_dot(beside_all[:, tap].reshape(-1, width), temporal_full[tap])
    denoised = (section.astype(jnp.float32) + total.reshape(latents.shape)).astype(jnp.bfloat16)

    groups = mine[0].shape[0]
    slots = cands * CAP
    spread_x = lax.axis_size("x")
    spread_y = lax.axis_size("y")
    raw = targets.reshape(-1)
    rel_y = (raw // spread_x - lax.axis_index("y") + 2) % spread_y
    rel_x = (raw % spread_x - lax.axis_index("x") + 2) % spread_x
    flat_targets = rel_y * spread_x + rel_x
    chosen = (flat_targets[:, None] == jnp.arange(groups, dtype=jnp.int32)[None, :]).astype(
        jnp.int32
    )
    earlier = jnp.cumsum(chosen, axis=0) - chosen
    slot_of = jnp.sum(earlier * chosen, axis=1)
    live = jnp.repeat(feasible.reshape(-1), IMG_ROWS) > 0
    position = flat_targets * slots + slot_of
    placing = (
        (jnp.arange(groups * slots, dtype=jnp.int32)[:, None] == position[None, :]) & live[None, :]
    ).astype(jnp.bfloat16)
    rows = denoised.reshape(cands * IMG_ROWS, IMG_COLS * width)
    block = (
        jnp.dot(placing, rows, preferred_element_type=jnp.float32)
        .astype(jnp.bfloat16)
        .reshape(groups, slots * IMG_COLS, width)
    )

    def slope_of(w, h):
        pre = jnp.einsum("gtc,gch->gth", block, w, preferred_element_type=jnp.float32)
        return ((1.0 - jnp.tanh(pre) ** 2) * h[:, None, :]).astype(jnp.bfloat16)

    grads = jnp.einsum(
        "gth,gch->gtc", slope_of(*mine), mine[0], preferred_element_type=jnp.float32
    ) + jnp.einsum(
        "gth,gch->gtc", slope_of(*other), other[0], preferred_element_type=jnp.float32
    )
    returned = grads.astype(jnp.bfloat16).reshape(groups * slots, -1)
    back = jnp.dot(placing.T, returned, preferred_element_type=jnp.float32)
    guided = (rows.astype(jnp.float32) - back).astype(jnp.bfloat16)
    return guided.reshape(latents.shape)


def solution(mesh):
    fine = Mesh(np.asarray(mesh.devices).reshape(8, 2, 4, 4), ("z", "c", "y", "x"))
    in_specs = (
        P(BATCH, FSDP, None, None),
        P(),
        P(),
        P(None, None, FSDP),
        P(None, None, FSDP),
        P(BATCH, None, None),
        P(BATCH, None),
        P(BATCH, None, None),
        P(BATCH, FSDP),
    )
    out_specs = P(BATCH, FSDP, None, None)
    return jax.shard_map(
        per_device, mesh=fine, in_specs=in_specs, out_specs=out_specs, check_vma=False
    )
```

```python
import jax
import jax.numpy as jnp
import numpy as np
from jax import lax
from jax.sharding import Mesh
from jax.sharding import PartitionSpec as P

GROUPS = 32
IMG_ROWS = 32
IMG_COLS = 32
PIX = 1024
CAP = 4
FSDP = ("z", "c")
BATCH = ("y", "x")
HEAD_ROWS = 8


def with_halo(array, axis, dim):
    size, length = (lax.axis_size(axis), array.shape[dim])
    up = [(i, (i + 1) % size) for i in range(size - 1)]
    down = [(j, i) for i, j in up]
    last = lax.slice_in_dim(array, length - 1, length, axis=dim)
    leading = lax.slice_in_dim(array, 0, 1, axis=dim)
    before = lax.ppermute(last, axis, up)
    after = lax.ppermute(leading, axis, down)
    return jnp.concatenate([before, array, after], axis=dim)


def group_silu(values, gain):
    shape = values.shape
    width = shape[-1]
    grouped = values.astype(jnp.float32).reshape(-1, shape[-2], GROUPS, width // GROUPS)
    center = jnp.mean(grouped, axis=(1, 3), keepdims=True)
    spread = jnp.mean((grouped - center) ** 2, axis=(1, 3), keepdims=True)
    normed = ((grouped - center) * lax.rsqrt(spread + 1e-05)).reshape(shape) * gain
    return jax.nn.silu(normed).astype(jnp.bfloat16)


def swap_cores(value):
    return lax.ppermute(value, "c", [(0, 1), (1, 0)])


def nt_dot(a, b):
    return lax.dot_general(a, b, (((1,), (1,)), ((), ())), preferred_element_type=jnp.float32)


def interleave(core, mine, other):
    p = mine.shape[0]
    parts = mine.shape[1] // 40
    a = mine.reshape(p, parts, 1, 40)
    b = other.reshape(p, parts, 1, 40)
    first = jnp.where(core == 0, a, b)
    second = jnp.where(core == 0, b, a)
    return jnp.concatenate([first, second], axis=2).reshape(p, -1)


def per_device(
    latents, norm_gain, second_gain, spatial_w, temporal_w, critic_w, critic_head, targets, feasible
):
    cands = latents.shape[0]
    width = latents.shape[-1]
    hid = critic_w.shape[-1]
    core = lax.axis_index("c")
    taps = spatial_w.shape[0]

    joint = jnp.swapaxes(jnp.concatenate([spatial_w, temporal_w], axis=0), 1, 2)
    joint_mine = lax.all_gather(joint, "z", axis=1, tiled=True)

    half = hid // 2
    own_w = lax.dynamic_slice_in_dim(critic_w[0], core * half, half, axis=1)
    own_h = lax.dynamic_slice_in_dim(critic_head[0], core * half, half, axis=0)
    hi = own_h.astype(jnp.bfloat16)
    rest = own_h - hi.astype(jnp.float32)
    mid = rest.astype(jnp.bfloat16)
    lo = (rest - mid.astype(jnp.float32)).astype(jnp.bfloat16)
    pad = jnp.zeros((HEAD_ROWS - 3, half), jnp.bfloat16)
    packed = jnp.concatenate([hi[None], mid[None], lo[None], pad, own_w], axis=0)
    packed, joint_mine = lax.optimization_barrier((packed, joint_mine))
    crit_mine = lax.all_gather(packed, BATCH, axis=0, tiled=False)

    joint_other = swap_cores(joint_mine)
    crit_other = swap_cores(crit_mine)

    first = group_silu(latents, norm_gain)
    padded = jnp.pad(
        first.reshape(cands, IMG_ROWS, IMG_COLS, width), ((0, 0), (1, 1), (1, 1), (0, 0))
    )
    acc_mine = jnp.zeros((cands * PIX, joint_mine.shape[1]), jnp.float32)
    acc_other = acc_mine
    for offset in range(taps):
        row_off, col_off = divmod(offset, 3)
        window = padded[:, row_off : row_off + IMG_ROWS, col_off : col_off + IMG_COLS].reshape(
            -1, width
        )
        acc_mine = acc_mine + nt_dot(window, joint_mine[offset])
        acc_other = acc_other + nt_dot(window, joint_other[offset])
    mixed = interleave(core, acc_mine, acc_other)
    section = (latents.astype(jnp.float32) + mixed.reshape(latents.shape)).astype(jnp.bfloat16)
    second = group_silu(section, second_gain)
    beside_all = with_halo(second, FSDP, 1)
    acc_mine = jnp.zeros((cands * PIX, joint_mine.shape[1]), jnp.float32)
    acc_other = acc_mine
    for tap in range(3):
        window = beside_all[:, tap].reshape(-1, width)
        acc_mine = acc_mine + nt_dot(window, joint_mine[taps + tap])
        acc_other = acc_other + nt_dot(window, joint_other[taps + tap])
    motion = interleave(core, acc_mine, acc_other)
    denoised = (section.astype(jnp.float32) + motion.reshape(latents.shape)).astype(jnp.bfloat16)

    groups = crit_mine.shape[0]
    slots = cands * CAP
    flat_targets = targets.reshape(-1)
    chosen = (flat_targets[:, None] == jnp.arange(groups, dtype=jnp.int32)[None, :]).astype(
        jnp.int32
    )
    earlier = jnp.cumsum(chosen, axis=0) - chosen
    slot_of = jnp.sum(earlier * chosen, axis=1)
    live = jnp.repeat(feasible.reshape(-1), IMG_ROWS) > 0
    position = flat_targets * slots + slot_of
    placing = (
        (jnp.arange(groups * slots, dtype=jnp.int32)[:, None] == position[None, :]) & live[None, :]
    ).astype(jnp.bfloat16)
    rows = denoised.reshape(cands * IMG_ROWS, IMG_COLS, width)
    block = (
        jnp.einsum("qr,rpc->qpc", placing, rows, preferred_element_type=jnp.float32)
        .astype(jnp.bfloat16)
        .reshape(groups, slots * IMG_COLS, width)
    )

    def grads_of(packed_all):
        heads = (
            packed_all[:, 0].astype(jnp.float32)
            + packed_all[:, 1].astype(jnp.float32)
            + packed_all[:, 2].astype(jnp.float32)
        )
        w = packed_all[:, HEAD_ROWS:]
        pre = jnp.einsum("gtc,gch->gth", block, w, preferred_element_type=jnp.float32)
        slope = ((1.0 - jnp.tanh(pre) ** 2) * heads[:, None, :]).astype(jnp.bfloat16)
        slope = lax.optimization_barrier(slope)
        return jnp.einsum("gth,gch->gtc", slope, w, preferred_element_type=jnp.float32)

    grads = (grads_of(crit_mine) + grads_of(crit_other)).astype(jnp.bfloat16)
    returned = grads.reshape(groups * slots, IMG_COLS, width)
    back = jnp.einsum("qr,qpc->rpc", placing, returned, preferred_element_type=jnp.float32)
    guided = (rows.astype(jnp.float32) - back).astype(jnp.bfloat16)
    return guided.reshape(latents.shape)


def solution(mesh):
    fine = Mesh(np.asarray(mesh.devices).reshape(8, 2, 4, 4), ("z", "c", "y", "x"))
    in_specs = (
        P(BATCH, FSDP, None, None),
        P(),
        P(),
        P(None, None, FSDP),
        P(None, None, FSDP),
        P(BATCH, None, None),
        P(BATCH, None),
        P(BATCH, None, None),
        P(BATCH, FSDP),
    )
    out_specs = P(BATCH, FSDP, None, None)
    return jax.shard_map(
        per_device, mesh=fine, in_specs=in_specs, out_specs=out_specs, check_vma=False
    )
```

```python
import jax
import jax.numpy as jnp
import numpy as np
from jax import lax
from jax.sharding import Mesh
from jax.sharding import PartitionSpec as P

GROUPS = 32
IMG_ROWS = 32
IMG_COLS = 32
PIX = 1024
CAP = 4
FSDP = ("z", "c")
BATCH = ("y", "x")


def with_halo(array, axis, dim):
    size, length = (lax.axis_size(axis), array.shape[dim])
    up = [(i, (i + 1) % size) for i in range(size - 1)]
    down = [(j, i) for i, j in up]
    last = lax.slice_in_dim(array, length - 1, length, axis=dim)
    leading = lax.slice_in_dim(array, 0, 1, axis=dim)
    before = lax.ppermute(last, axis, up)
    after = lax.ppermute(leading, axis, down)
    return jnp.concatenate([before, array, after], axis=dim)


def group_silu(values, gain):
    shape = values.shape
    width = shape[-1]
    grouped = values.astype(jnp.float32).reshape(-1, shape[-2], GROUPS, width // GROUPS)
    center = jnp.mean(grouped, axis=(1, 3), keepdims=True)
    spread = jnp.mean((grouped - center) ** 2, axis=(1, 3), keepdims=True)
    normed = ((grouped - center) * lax.rsqrt(spread + 1e-05)).reshape(shape) * gain
    return jax.nn.silu(normed).astype(jnp.bfloat16)


def gather_out_major(weights):
    turned = jnp.swapaxes(weights, 1, 2)
    return lax.all_gather(turned, FSDP, axis=1, tiled=True)


def ring_gather(parts, axis):
    size = lax.axis_size(axis)
    fwd = [(i, (i + 1) % size) for i in range(size)]
    bwd = [(i, (i - 1) % size) for i in range(size)]
    out = []
    for v in parts:
        from_m1 = lax.ppermute(v, axis, fwd)
        from_p1 = lax.ppermute(v, axis, bwd)
        cut = v.shape[-1] // 2
        left = lax.ppermute(from_m1[..., :cut], axis, fwd)
        right = lax.ppermute(from_p1[..., cut:], axis, bwd)
        from_m2 = jnp.concatenate([left, right], axis=-1)
        out.append(jnp.stack([from_m2, from_m1, v, from_p1]))
    return tuple(out)


def nt_dot(a, b):
    return lax.dot_general(a, b, (((1,), (1,)), ((), ())), preferred_element_type=jnp.float32)


def per_device(
    latents, norm_gain, second_gain, spatial_w, temporal_w, critic_w, critic_head, targets, feasible
):
    cands = latents.shape[0]
    width = latents.shape[-1]
    hid = critic_w.shape[-1]

    core = lax.axis_index("c")
    half = hid // 2
    own = (
        lax.dynamic_slice_in_dim(critic_w[0], core * half, half, axis=1),
        lax.dynamic_slice_in_dim(critic_head[0], core * half, half, axis=0),
    )
    cut = half // 2
    first_x = ring_gather(tuple(v[..., :cut] for v in own), "x")
    first_x = ring_gather(first_x, "y")
    first_y = ring_gather(tuple(v[..., cut:] for v in own), "y")
    first_y = ring_gather(first_y, "x")
    mine = tuple(
        jnp.concatenate([a, jnp.swapaxes(b, 0, 1)], axis=-1).reshape(-1, *a.shape[2:-1], 2 * cut)
        for a, b in zip(first_x, first_y)
    )
    other = tuple(lax.ppermute(m, "c", [(0, 1), (1, 0)]) for m in mine)

    joint = jnp.concatenate([spatial_w, temporal_w], axis=0)
    joint_full = gather_out_major(joint)
    spatial_full = joint_full[: spatial_w.shape[0]]
    temporal_full = joint_full[spatial_w.shape[0] :]

    first = group_silu(latents, norm_gain)
    padded = jnp.pad(
        first.reshape(cands, IMG_ROWS, IMG_COLS, width), ((0, 0), (1, 1), (1, 1), (0, 0))
    )
    total = jnp.zeros((cands * PIX, spatial_full.shape[1]), jnp.float32)
    for offset in range(9):
        row_off, col_off = divmod(offset, 3)
        window = padded[:, row_off : row_off + IMG_ROWS, col_off : col_off + IMG_COLS].reshape(
            -1, width
        )
        total = total + nt_dot(window, spatial_full[offset])
    section = (latents.astype(jnp.float32) + total.reshape(latents.shape)).astype(jnp.bfloat16)
    second = group_silu(section, second_gain)
    beside_all = with_halo(second, FSDP, 1)
    total = jnp.zeros((cands * PIX, temporal_full.shape[1]), jnp.float32)
    for tap in range(3):
        total = total + nt_dot(beside_all[:, tap].reshape(-1, width), temporal_full[tap])
    denoised = (section.astype(jnp.float32) + total.reshape(latents.shape)).astype(jnp.bfloat16)

    groups = mine[0].shape[0]
    slots = cands * CAP
    spread_x = lax.axis_size("x")
    spread_y = lax.axis_size("y")
    raw = targets.reshape(-1)
    rel_y = (raw // spread_x - lax.axis_index("y") + 2) % spread_y
    rel_x = (raw % spread_x - lax.axis_index("x") + 2) % spread_x
    flat_targets = rel_y * spread_x + rel_x
    chosen = (flat_targets[:, None] == jnp.arange(groups, dtype=jnp.int32)[None, :]).astype(
        jnp.int32
    )
    earlier = jnp.cumsum(chosen, axis=0) - chosen
    slot_of = jnp.sum(earlier * chosen, axis=1)
    live = jnp.repeat(feasible.reshape(-1), IMG_ROWS) > 0
    position = flat_targets * slots + slot_of
    placing = (
        (jnp.arange(groups * slots, dtype=jnp.int32)[:, None] == position[None, :]) & live[None, :]
    ).astype(jnp.bfloat16)
    rows = denoised.reshape(cands * IMG_ROWS, IMG_COLS, width)
    block = (
        jnp.einsum("qr,rpc->qpc", placing, rows, preferred_element_type=jnp.float32)
        .astype(jnp.bfloat16)
        .reshape(groups, slots * IMG_COLS, width)
    )

    def slope_of(w, h):
        pre = jnp.einsum("gtc,gch->gth", block, w, preferred_element_type=jnp.float32)
        return ((1.0 - jnp.tanh(pre) ** 2) * h[:, None, :]).astype(jnp.bfloat16)

    grads = jnp.einsum(
        "gth,gch->gtc", slope_of(*mine), mine[0], preferred_element_type=jnp.float32
    ) + jnp.einsum(
        "gth,gch->gtc", slope_of(*other), other[0], preferred_element_type=jnp.float32
    )
    returned = grads.astype(jnp.bfloat16).reshape(groups * slots, IMG_COLS, width)
    back = jnp.einsum("qr,qpc->rpc", placing, returned, preferred_element_type=jnp.float32)
    guided = (rows.astype(jnp.float32) - back).astype(jnp.bfloat16)
    return guided.reshape(latents.shape)


def solution(mesh):
    fine = Mesh(np.asarray(mesh.devices).reshape(8, 2, 4, 4), ("z", "c", "y", "x"))
    in_specs = (
        P(BATCH, FSDP, None, None),
        P(),
        P(),
        P(None, None, FSDP),
        P(None, None, FSDP),
        P(BATCH, None, None),
        P(BATCH, None),
        P(BATCH, None, None),
        P(BATCH, FSDP),
    )
    out_specs = P(BATCH, FSDP, None, None)
    return jax.shard_map(
        per_device, mesh=fine, in_specs=in_specs, out_specs=out_specs, check_vma=False
    )
```

```python
import jax
import jax.numpy as jnp
import numpy as np
from jax import lax
from jax.experimental import pallas as pl
from jax.sharding import Mesh
from jax.sharding import PartitionSpec as P

GROUPS = 32
IMG_ROWS = 32
IMG_COLS = 32
PIX = 1024
CAP = 4
FSDP = ("z", "c")
HEAD_ROWS = 8
BATCH = ("y", "x")


def with_halo(array, axis, dim):
    size, length = (lax.axis_size(axis), array.shape[dim])
    up = [(i, (i + 1) % size) for i in range(size - 1)]
    down = [(j, i) for i, j in up]
    last = lax.slice_in_dim(array, length - 1, length, axis=dim)
    leading = lax.slice_in_dim(array, 0, 1, axis=dim)
    before = lax.ppermute(last, axis, up)
    after = lax.ppermute(leading, axis, down)
    return jnp.concatenate([before, array, after], axis=dim)


def group_silu(values, gain):
    shape = values.shape
    width = shape[-1]
    grouped = values.astype(jnp.float32).reshape(-1, shape[-2], GROUPS, width // GROUPS)
    center = jnp.mean(grouped, axis=(1, 3), keepdims=True)
    spread = jnp.mean((grouped - center) ** 2, axis=(1, 3), keepdims=True)
    normed = ((grouped - center) * lax.rsqrt(spread + 1e-05)).reshape(shape) * gain
    return jax.nn.silu(normed).astype(jnp.bfloat16)


def gather_out_major(weights):
    turned = jnp.swapaxes(weights, 1, 2)
    return lax.all_gather(turned, FSDP, axis=1, tiled=True)


def ring_gather(parts, axis):
    size = lax.axis_size(axis)
    fwd = [(i, (i + 1) % size) for i in range(size)]
    bwd = [(i, (i - 1) % size) for i in range(size)]
    out = []
    for v in parts:
        from_m1 = lax.ppermute(v, axis, fwd)
        from_p1 = lax.ppermute(v, axis, bwd)
        cut = v.shape[-1] // 2
        left = lax.ppermute(from_m1[..., :cut], axis, fwd)
        right = lax.ppermute(from_p1[..., cut:], axis, bwd)
        from_m2 = jnp.concatenate([left, right], axis=-1)
        out.append(jnp.stack([from_m2, from_m1, v, from_p1]))
    return tuple(out)


def critic_kernel(block_ref, mine_ref, other_ref, out_ref):
    rows = block_ref[0]

    def part(packed_ref):
        w = packed_ref[0, HEAD_ROWS:, :]
        heads = (
            packed_ref[0, 0:1, :].astype(jnp.float32)
            + packed_ref[0, 1:2, :].astype(jnp.float32)
            + packed_ref[0, 2:3, :].astype(jnp.float32)
        )
        pre = jnp.dot(rows, w, preferred_element_type=jnp.float32)
        lean = jnp.tanh(pre)
        slope = ((1.0 - lean * lean) * heads).astype(jnp.bfloat16)
        return lax.dot_general(
            slope, w, (((1,), (1,)), ((), ())), preferred_element_type=jnp.float32
        )

    out_ref[0] = (part(mine_ref) + part(other_ref)).astype(out_ref.dtype)


def critic_grads(block, mine, other):
    groups, count, width = block.shape
    packed_rows, half = mine.shape[1:]
    return pl.pallas_call(
        critic_kernel,
        grid=(groups,),
        in_specs=[
            pl.BlockSpec((1, count, width), lambda g: (g, 0, 0)),
            pl.BlockSpec((1, packed_rows, half), lambda g: (g, 0, 0)),
            pl.BlockSpec((1, packed_rows, half), lambda g: (g, 0, 0)),
        ],
        out_specs=pl.BlockSpec((1, count, width), lambda g: (g, 0, 0)),
        out_shape=jax.ShapeDtypeStruct(block.shape, jnp.bfloat16),
    )(block, mine, other)


def nt_dot(a, b):
    return lax.dot_general(a, b, (((1,), (1,)), ((), ())), preferred_element_type=jnp.float32)


def per_device(
    latents, norm_gain, second_gain, spatial_w, temporal_w, critic_w, critic_head, targets, feasible
):
    cands = latents.shape[0]
    width = latents.shape[-1]
    hid = critic_w.shape[-1]

    core = lax.axis_index("c")
    half = hid // 2
    own_w = lax.dynamic_slice_in_dim(critic_w[0], core * half, half, axis=1)
    own_h = lax.dynamic_slice_in_dim(critic_head[0], core * half, half, axis=0)
    hi = own_h.astype(jnp.bfloat16)
    rest = own_h - hi.astype(jnp.float32)
    mid = rest.astype(jnp.bfloat16)
    lo = (rest - mid.astype(jnp.float32)).astype(jnp.bfloat16)
    pad = jnp.zeros((HEAD_ROWS - 3, half), jnp.bfloat16)
    own = (jnp.concatenate([hi[None], mid[None], lo[None], pad, own_w], axis=0),)
    cut = half // 2
    first_x = ring_gather(tuple(v[..., :cut] for v in own), "x")
    first_x = ring_gather(first_x, "y")
    first_y = ring_gather(tuple(v[..., cut:] for v in own), "y")
    first_y = ring_gather(first_y, "x")
    mine = tuple(
        jnp.concatenate([a, jnp.swapaxes(b, 0, 1)], axis=-1).reshape(-1, *a.shape[2:-1], 2 * cut)
        for a, b in zip(first_x, first_y)
    )
    other = tuple(lax.ppermute(m, "c", [(0, 1), (1, 0)]) for m in mine)

    joint = jnp.concatenate([spatial_w, temporal_w], axis=0)
    joint_full = gather_out_major(joint)
    spatial_full = joint_full[: spatial_w.shape[0]]
    temporal_full = joint_full[spatial_w.shape[0] :]

    first = group_silu(latents, norm_gain)
    padded = jnp.pad(
        first.reshape(cands, IMG_ROWS, IMG_COLS, width), ((0, 0), (1, 1), (1, 1), (0, 0))
    )
    total = jnp.zeros((cands * PIX, spatial_full.shape[1]), jnp.float32)
    for offset in range(9):
        row_off, col_off = divmod(offset, 3)
        window = padded[:, row_off : row_off + IMG_ROWS, col_off : col_off + IMG_COLS].reshape(
            -1, width
        )
        total = total + nt_dot(window, spatial_full[offset])
    section = (latents.astype(jnp.float32) + total.reshape(latents.shape)).astype(jnp.bfloat16)
    second = group_silu(section, second_gain)
    beside_all = with_halo(second, FSDP, 1)
    total = jnp.zeros((cands * PIX, temporal_full.shape[1]), jnp.float32)
    for tap in range(3):
        total = total + nt_dot(beside_all[:, tap].reshape(-1, width), temporal_full[tap])
    denoised = (section.astype(jnp.float32) + total.reshape(latents.shape)).astype(jnp.bfloat16)

    groups = mine[0].shape[0]
    slots = cands * CAP
    spread_x = lax.axis_size("x")
    spread_y = lax.axis_size("y")
    raw = targets.reshape(-1)
    rel_y = (raw // spread_x - lax.axis_index("y") + 2) % spread_y
    rel_x = (raw % spread_x - lax.axis_index("x") + 2) % spread_x
    flat_targets = rel_y * spread_x + rel_x
    chosen = (flat_targets[:, None] == jnp.arange(groups, dtype=jnp.int32)[None, :]).astype(
        jnp.int32
    )
    earlier = jnp.cumsum(chosen, axis=0) - chosen
    slot_of = jnp.sum(earlier * chosen, axis=1)
    live = jnp.repeat(feasible.reshape(-1), IMG_ROWS) > 0
    position = flat_targets * slots + slot_of
    placing = (
        (jnp.arange(groups * slots, dtype=jnp.int32)[:, None] == position[None, :]) & live[None, :]
    ).astype(jnp.bfloat16)
    rows = denoised.reshape(cands * IMG_ROWS, IMG_COLS, width)
    block = (
        jnp.einsum("qr,rpc->qpc", placing, rows, preferred_element_type=jnp.float32)
        .astype(jnp.bfloat16)
        .reshape(groups, slots * IMG_COLS, width)
    )

    grads = critic_grads(block, mine[0], other[0])
    returned = grads.reshape(groups * slots, IMG_COLS, width)
    back = jnp.einsum("qr,qpc->rpc", placing, returned, preferred_element_type=jnp.float32)
    guided = (rows.astype(jnp.float32) - back).astype(jnp.bfloat16)
    return guided.reshape(latents.shape)


def solution(mesh):
    fine = Mesh(np.asarray(mesh.devices).reshape(8, 2, 4, 4), ("z", "c", "y", "x"))
    in_specs = (
        P(BATCH, FSDP, None, None),
        P(),
        P(),
        P(None, None, FSDP),
        P(None, None, FSDP),
        P(BATCH, None, None),
        P(BATCH, None),
        P(BATCH, None, None),
        P(BATCH, FSDP),
    )
    out_specs = P(BATCH, FSDP, None, None)
    return jax.shard_map(
        per_device, mesh=fine, in_specs=in_specs, out_specs=out_specs, check_vma=False
    )
```

```python
import jax
import jax.numpy as jnp
import numpy as np
from jax import lax
from jax.sharding import Mesh
from jax.sharding import PartitionSpec as P

GROUPS = 32
IMG_ROWS = 32
IMG_COLS = 32
PIX = 1024
CAP = 4
FSDP = ("z", "c")
HEAD_ROWS = 8
BATCH = ("y", "x")


def with_halo(array, axis, dim):
    size, length = (lax.axis_size(axis), array.shape[dim])
    up = [(i, (i + 1) % size) for i in range(size - 1)]
    down = [(j, i) for i, j in up]
    last = lax.slice_in_dim(array, length - 1, length, axis=dim)
    leading = lax.slice_in_dim(array, 0, 1, axis=dim)
    before = lax.ppermute(last, axis, up)
    after = lax.ppermute(leading, axis, down)
    return jnp.concatenate([before, array, after], axis=dim)


def group_silu(values, gain):
    shape = values.shape
    width = shape[-1]
    grouped = values.astype(jnp.float32).reshape(-1, shape[-2], GROUPS, width // GROUPS)
    center = jnp.mean(grouped, axis=(1, 3), keepdims=True)
    spread = jnp.mean((grouped - center) ** 2, axis=(1, 3), keepdims=True)
    normed = ((grouped - center) * lax.rsqrt(spread + 1e-05)).reshape(shape) * gain
    return jax.nn.silu(normed).astype(jnp.bfloat16)


def gather_out_major(weights):
    turned = jnp.swapaxes(weights, 1, 2)
    return lax.all_gather(turned, FSDP, axis=1, tiled=True)


def ring_gather(parts, axis):
    size = lax.axis_size(axis)
    fwd = [(i, (i + 1) % size) for i in range(size)]
    bwd = [(i, (i - 1) % size) for i in range(size)]
    out = []
    for v in parts:
        from_m1 = lax.ppermute(v, axis, fwd)
        from_p1 = lax.ppermute(v, axis, bwd)
        cut = v.shape[-1] // 2
        left = lax.ppermute(from_m1[..., :cut], axis, fwd)
        right = lax.ppermute(from_p1[..., cut:], axis, bwd)
        from_m2 = jnp.concatenate([left, right], axis=-1)
        out.append(jnp.stack([from_m2, from_m1, v, from_p1]))
    return tuple(out)


def nt_dot(a, b):
    return lax.dot_general(a, b, (((1,), (1,)), ((), ())), preferred_element_type=jnp.float32)


def per_device(
    latents, norm_gain, second_gain, spatial_w, temporal_w, critic_w, critic_head, targets, feasible
):
    cands = latents.shape[0]
    width = latents.shape[-1]
    hid = critic_w.shape[-1]

    core = lax.axis_index("c")
    half = hid // 2
    own_w = lax.dynamic_slice_in_dim(critic_w[0], core * half, half, axis=1)
    own_h = lax.dynamic_slice_in_dim(critic_head[0], core * half, half, axis=0)
    hi = own_h.astype(jnp.bfloat16)
    rest = own_h - hi.astype(jnp.float32)
    mid = rest.astype(jnp.bfloat16)
    lo = (rest - mid.astype(jnp.float32)).astype(jnp.bfloat16)
    pad = jnp.zeros((HEAD_ROWS - 3, half), jnp.bfloat16)
    own = (jnp.concatenate([hi[None], mid[None], lo[None], pad, own_w], axis=0),)
    cut = half // 2
    first_x = ring_gather(tuple(v[..., :cut] for v in own), "x")
    first_x = ring_gather(first_x, "y")
    first_y = ring_gather(tuple(v[..., cut:] for v in own), "y")
    first_y = ring_gather(first_y, "x")
    mine = tuple(
        jnp.concatenate([a, jnp.swapaxes(b, 0, 1)], axis=-1).reshape(-1, *a.shape[2:-1], 2 * cut)
        for a, b in zip(first_x, first_y)
    )
    other = tuple(lax.ppermute(m, "c", [(0, 1), (1, 0)]) for m in mine)

    joint = jnp.concatenate([spatial_w, temporal_w], axis=0)
    joint_full = gather_out_major(joint)
    spatial_full = joint_full[: spatial_w.shape[0]]
    temporal_full = joint_full[spatial_w.shape[0] :]

    first = group_silu(latents, norm_gain)
    padded = jnp.pad(
        first.reshape(cands, IMG_ROWS, IMG_COLS, width), ((0, 0), (1, 1), (1, 1), (0, 0))
    )
    total = jnp.zeros((cands * PIX, spatial_full.shape[1]), jnp.float32)
    for offset in range(9):
        row_off, col_off = divmod(offset, 3)
        window = padded[:, row_off : row_off + IMG_ROWS, col_off : col_off + IMG_COLS].reshape(
            -1, width
        )
        total = total + nt_dot(window, spatial_full[offset])
    section = (latents.astype(jnp.float32) + total.reshape(latents.shape)).astype(jnp.bfloat16)
    second = group_silu(section, second_gain)
    beside_all = with_halo(second, FSDP, 1)
    total = jnp.zeros((cands * PIX, temporal_full.shape[1]), jnp.float32)
    for tap in range(3):
        total = total + nt_dot(beside_all[:, tap].reshape(-1, width), temporal_full[tap])
    denoised = (section.astype(jnp.float32) + total.reshape(latents.shape)).astype(jnp.bfloat16)

    groups = mine[0].shape[0]
    slots = cands * CAP
    spread_x = lax.axis_size("x")
    spread_y = lax.axis_size("y")
    raw = targets.reshape(-1)
    rel_y = (raw // spread_x - lax.axis_index("y") + 2) % spread_y
    rel_x = (raw % spread_x - lax.axis_index("x") + 2) % spread_x
    flat_targets = rel_y * spread_x + rel_x
    chosen = (flat_targets[:, None] == jnp.arange(groups, dtype=jnp.int32)[None, :]).astype(
        jnp.int32
    )
    earlier = jnp.cumsum(chosen, axis=0) - chosen
    slot_of = jnp.sum(earlier * chosen, axis=1)
    live = jnp.repeat(feasible.reshape(-1), IMG_ROWS) > 0
    position = flat_targets * slots + slot_of
    placing = (
        (jnp.arange(groups * slots, dtype=jnp.int32)[:, None] == position[None, :]) & live[None, :]
    ).astype(jnp.bfloat16)
    rows = denoised.reshape(cands * IMG_ROWS, IMG_COLS, width)
    block = (
        jnp.einsum("qr,rpc->qpc", placing, rows, preferred_element_type=jnp.float32)
        .astype(jnp.bfloat16)
        .reshape(groups, slots * IMG_COLS, width)
    )

    def grads_of(packed_all):
        heads = (
            packed_all[:, 0].astype(jnp.float32)
            + packed_all[:, 1].astype(jnp.float32)
            + packed_all[:, 2].astype(jnp.float32)
        )
        w = packed_all[:, HEAD_ROWS:]
        pre = jnp.einsum("gtc,gch->gth", block, w, preferred_element_type=jnp.float32)
        slope = ((1.0 - jnp.tanh(pre) ** 2) * heads[:, None, :]).astype(jnp.bfloat16)
        return jnp.einsum("gth,gch->gtc", slope, w, preferred_element_type=jnp.float32)

    grads = (grads_of(mine[0]) + grads_of(other[0])).astype(jnp.bfloat16)
    returned = grads.reshape(groups * slots, IMG_COLS, width)
    back = jnp.einsum("qr,qpc->rpc", placing, returned, preferred_element_type=jnp.float32)
    guided = (rows.astype(jnp.float32) - back).astype(jnp.bfloat16)
    return guided.reshape(latents.shape)


def solution(mesh):
    fine = Mesh(np.asarray(mesh.devices).reshape(8, 2, 4, 4), ("z", "c", "y", "x"))
    in_specs = (
        P(BATCH, FSDP, None, None),
        P(),
        P(),
        P(None, None, FSDP),
        P(None, None, FSDP),
        P(BATCH, None, None),
        P(BATCH, None),
        P(BATCH, None, None),
        P(BATCH, FSDP),
    )
    out_specs = P(BATCH, FSDP, None, None)
    return jax.shard_map(
        per_device, mesh=fine, in_specs=in_specs, out_specs=out_specs, check_vma=False
    )
```

```python
import jax
import jax.numpy as jnp
import numpy as np
from jax import lax
from jax.sharding import Mesh
from jax.sharding import PartitionSpec as P

GROUPS = 32
IMG_ROWS = 32
IMG_COLS = 32
PIX = 1024
CAP = 4
FSDP = ("z", "c")
HEAD_ROWS = 8
BATCH = ("y", "x")


def with_halo(array, axis, dim):
    size, length = (lax.axis_size(axis), array.shape[dim])
    up = [(i, (i + 1) % size) for i in range(size - 1)]
    down = [(j, i) for i, j in up]
    last = lax.slice_in_dim(array, length - 1, length, axis=dim)
    leading = lax.slice_in_dim(array, 0, 1, axis=dim)
    before = lax.ppermute(last, axis, up)
    after = lax.ppermute(leading, axis, down)
    return jnp.concatenate([before, array, after], axis=dim)


def group_silu(values, gain):
    shape = values.shape
    width = shape[-1]
    grouped = values.astype(jnp.float32).reshape(-1, shape[-2], GROUPS, width // GROUPS)
    center = jnp.mean(grouped, axis=(1, 3), keepdims=True)
    spread = jnp.mean((grouped - center) ** 2, axis=(1, 3), keepdims=True)
    normed = ((grouped - center) * lax.rsqrt(spread + 1e-05)).reshape(shape) * gain
    return jax.nn.silu(normed).astype(jnp.bfloat16)


def gather_out_major(weights):
    turned = jnp.swapaxes(weights, 1, 2)
    return lax.all_gather(turned, FSDP, axis=1, tiled=True)


def ring_gather(parts, axis):
    size = lax.axis_size(axis)
    fwd = [(i, (i + 1) % size) for i in range(size)]
    bwd = [(i, (i - 1) % size) for i in range(size)]
    out = []
    for v in parts:
        from_m1 = lax.ppermute(v, axis, fwd)
        from_p1 = lax.ppermute(v, axis, bwd)
        cut = v.shape[-1] // 2
        left = lax.ppermute(from_m1[..., :cut], axis, fwd)
        right = lax.ppermute(from_p1[..., cut:], axis, bwd)
        from_m2 = jnp.concatenate([left, right], axis=-1)
        out.append(jnp.stack([from_m2, from_m1, v, from_p1]))
    return tuple(out)


def tap_dot(windows, weights):
    return lax.dot_general(
        windows, weights, (((1, 2), (0, 2)), ((), ())), preferred_element_type=jnp.float32
    )


def nt_dot(a, b):
    return lax.dot_general(a, b, (((1,), (1,)), ((), ())), preferred_element_type=jnp.float32)


def per_device(
    latents, norm_gain, second_gain, spatial_w, temporal_w, critic_w, critic_head, targets, feasible
):
    cands = latents.shape[0]
    width = latents.shape[-1]
    hid = critic_w.shape[-1]

    core = lax.axis_index("c")
    half = hid // 2
    own_w = lax.dynamic_slice_in_dim(critic_w[0], core * half, half, axis=1)
    own_h = lax.dynamic_slice_in_dim(critic_head[0], core * half, half, axis=0)
    hi = own_h.astype(jnp.bfloat16)
    rest = own_h - hi.astype(jnp.float32)
    mid = rest.astype(jnp.bfloat16)
    lo = (rest - mid.astype(jnp.float32)).astype(jnp.bfloat16)
    pad = jnp.zeros((HEAD_ROWS - 3, half), jnp.bfloat16)
    own = (jnp.concatenate([hi[None], mid[None], lo[None], pad, own_w], axis=0),)
    cut = half // 2
    first_x = ring_gather(tuple(v[..., :cut] for v in own), "x")
    first_x = ring_gather(first_x, "y")
    first_y = ring_gather(tuple(v[..., cut:] for v in own), "y")
    first_y = ring_gather(first_y, "x")
    mine = tuple(
        jnp.concatenate([a, jnp.swapaxes(b, 0, 1)], axis=-1).reshape(-1, *a.shape[2:-1], 2 * cut)
        for a, b in zip(first_x, first_y)
    )
    other = tuple(lax.ppermute(m, "c", [(0, 1), (1, 0)]) for m in mine)

    joint = jnp.concatenate([spatial_w, temporal_w], axis=0)
    joint_full = gather_out_major(joint)
    spatial_full = joint_full[: spatial_w.shape[0]]
    temporal_full = joint_full[spatial_w.shape[0] :]

    first = group_silu(latents, norm_gain)
    padded = jnp.pad(
        first.reshape(cands, IMG_ROWS, IMG_COLS, width), ((0, 0), (1, 1), (1, 1), (0, 0))
    )
    windows = jnp.stack(
        [
            padded[:, r : r + IMG_ROWS, q : q + IMG_COLS].reshape(-1, width)
            for r, q in (divmod(offset, 3) for offset in range(spatial_full.shape[0]))
        ],
        axis=1,
    )
    total = tap_dot(windows, spatial_full)
    section = (latents.astype(jnp.float32) + total.reshape(latents.shape)).astype(jnp.bfloat16)
    second = group_silu(section, second_gain)
    beside_all = with_halo(second, FSDP, 1)
    frames = jnp.moveaxis(beside_all, 1, 2).reshape(-1, temporal_full.shape[0], width)
    total = tap_dot(frames, temporal_full)
    denoised = (section.astype(jnp.float32) + total.reshape(latents.shape)).astype(jnp.bfloat16)

    groups = mine[0].shape[0]
    slots = cands * CAP
    spread_x = lax.axis_size("x")
    spread_y = lax.axis_size("y")
    raw = targets.reshape(-1)
    rel_y = (raw // spread_x - lax.axis_index("y") + 2) % spread_y
    rel_x = (raw % spread_x - lax.axis_index("x") + 2) % spread_x
    flat_targets = rel_y * spread_x + rel_x
    chosen = (flat_targets[:, None] == jnp.arange(groups, dtype=jnp.int32)[None, :]).astype(
        jnp.int32
    )
    earlier = jnp.cumsum(chosen, axis=0) - chosen
    slot_of = jnp.sum(earlier * chosen, axis=1)
    live = jnp.repeat(feasible.reshape(-1), IMG_ROWS) > 0
    position = flat_targets * slots + slot_of
    placing = (
        (jnp.arange(groups * slots, dtype=jnp.int32)[:, None] == position[None, :]) & live[None, :]
    ).astype(jnp.bfloat16)
    rows = denoised.reshape(cands * IMG_ROWS, IMG_COLS, width)
    block = (
        jnp.einsum("qr,rpc->qpc", placing, rows, preferred_element_type=jnp.float32)
        .astype(jnp.bfloat16)
        .reshape(groups, slots * IMG_COLS, width)
    )

    def grads_of(packed_all):
        heads = (
            packed_all[:, 0].astype(jnp.float32)
            + packed_all[:, 1].astype(jnp.float32)
            + packed_all[:, 2].astype(jnp.float32)
        )
        w = packed_all[:, HEAD_ROWS:]
        pre = jnp.einsum("gtc,gch->gth", block, w, preferred_element_type=jnp.float32)
        slope = ((1.0 - jnp.tanh(pre) ** 2) * heads[:, None, :]).astype(jnp.bfloat16)
        return jnp.einsum("gth,gch->gtc", slope, w, preferred_element_type=jnp.float32)

    grads = (grads_of(mine[0]) + grads_of(other[0])).astype(jnp.bfloat16)
    returned = grads.reshape(groups * slots, IMG_COLS, width)
    back = jnp.einsum("qr,qpc->rpc", placing, returned, preferred_element_type=jnp.float32)
    guided = (rows.astype(jnp.float32) - back).astype(jnp.bfloat16)
    return guided.reshape(latents.shape)


def solution(mesh):
    fine = Mesh(np.asarray(mesh.devices).reshape(8, 2, 4, 4), ("z", "c", "y", "x"))
    in_specs = (
        P(BATCH, FSDP, None, None),
        P(),
        P(),
        P(None, None, FSDP),
        P(None, None, FSDP),
        P(BATCH, None, None),
        P(BATCH, None),
        P(BATCH, None, None),
        P(BATCH, FSDP),
    )
    out_specs = P(BATCH, FSDP, None, None)
    return jax.shard_map(
        per_device, mesh=fine, in_specs=in_specs, out_specs=out_specs, check_vma=False
    )
```

```python
import jax
import jax.numpy as jnp
import numpy as np
from jax import lax
from jax.sharding import Mesh
from jax.sharding import PartitionSpec as P

GROUPS = 32
IMG_ROWS = 32
IMG_COLS = 32
PIX = 1024
CAP = 4
FSDP = ("z", "c")
HEAD_ROWS = 8
BATCH = ("y", "x")


def with_halo(array, axis, dim):
    size, length = (lax.axis_size(axis), array.shape[dim])
    up = [(i, (i + 1) % size) for i in range(size - 1)]
    down = [(j, i) for i, j in up]
    last = lax.slice_in_dim(array, length - 1, length, axis=dim)
    leading = lax.slice_in_dim(array, 0, 1, axis=dim)
    before = lax.ppermute(last, axis, up)
    after = lax.ppermute(leading, axis, down)
    return jnp.concatenate([before, array, after], axis=dim)


def group_silu(values, gain):
    shape = values.shape
    width = shape[-1]
    grouped = values.astype(jnp.float32).reshape(-1, shape[-2], GROUPS, width // GROUPS)
    center = jnp.mean(grouped, axis=(1, 3), keepdims=True)
    spread = jnp.mean((grouped - center) ** 2, axis=(1, 3), keepdims=True)
    normed = ((grouped - center) * lax.rsqrt(spread + 1e-05)).reshape(shape) * gain
    return jax.nn.silu(normed).astype(jnp.bfloat16)


def gather_out_major(weights):
    turned = jnp.swapaxes(weights, 1, 2)
    return lax.all_gather(turned, FSDP, axis=1, tiled=True)


def ring_gather(parts, axis):
    size = lax.axis_size(axis)
    fwd = [(i, (i + 1) % size) for i in range(size)]
    bwd = [(i, (i - 1) % size) for i in range(size)]
    out = []
    for v in parts:
        from_m1 = lax.ppermute(v, axis, fwd)
        from_p1 = lax.ppermute(v, axis, bwd)
        cut = v.shape[-1] // 2
        left = lax.ppermute(from_m1[..., :cut], axis, fwd)
        right = lax.ppermute(from_p1[..., cut:], axis, bwd)
        from_m2 = jnp.concatenate([left, right], axis=-1)
        out.append(jnp.stack([from_m2, from_m1, v, from_p1]))
    return tuple(out)


def tap_dot(windows, weights):
    return lax.dot_general(
        windows, weights, (((1, 2), (0, 2)), ((), ())), preferred_element_type=jnp.float32
    )


def nt_dot(a, b):
    return lax.dot_general(a, b, (((1,), (1,)), ((), ())), preferred_element_type=jnp.float32)


def per_device(
    latents, norm_gain, second_gain, spatial_w, temporal_w, critic_w, critic_head, targets, feasible
):
    cands = latents.shape[0]
    width = latents.shape[-1]
    hid = critic_w.shape[-1]

    core = lax.axis_index("c")
    half = hid // 2
    own_w = lax.dynamic_slice_in_dim(critic_w[0], core * half, half, axis=1)
    own_h = lax.dynamic_slice_in_dim(critic_head[0], core * half, half, axis=0)
    hi = own_h.astype(jnp.bfloat16)
    rest = own_h - hi.astype(jnp.float32)
    mid = rest.astype(jnp.bfloat16)
    lo = (rest - mid.astype(jnp.float32)).astype(jnp.bfloat16)
    pad = jnp.zeros((HEAD_ROWS - 3, half), jnp.bfloat16)
    own = (jnp.concatenate([own_w, hi[None], mid[None], lo[None], pad], axis=0),)
    cut = half // 2
    first_x = ring_gather(tuple(v[..., :cut] for v in own), "x")
    first_x = ring_gather(first_x, "y")
    first_y = ring_gather(tuple(v[..., cut:] for v in own), "y")
    first_y = ring_gather(first_y, "x")
    mine = tuple(
        jnp.concatenate([a, jnp.swapaxes(b, 0, 1)], axis=-1).reshape(-1, *a.shape[2:-1], 2 * cut)
        for a, b in zip(first_x, first_y)
    )
    other = tuple(lax.ppermute(m, "c", [(0, 1), (1, 0)]) for m in mine)

    joint = jnp.concatenate([spatial_w, temporal_w], axis=0)
    joint_full = gather_out_major(joint)
    spatial_full = joint_full[: spatial_w.shape[0]]
    temporal_full = joint_full[spatial_w.shape[0] :]

    first = group_silu(latents, norm_gain)
    padded = jnp.pad(
        first.reshape(cands, IMG_ROWS, IMG_COLS, width), ((0, 0), (1, 1), (1, 1), (0, 0))
    )
    windows = jnp.stack(
        [
            padded[:, r : r + IMG_ROWS, q : q + IMG_COLS].reshape(-1, width)
            for r, q in (divmod(offset, 3) for offset in range(spatial_full.shape[0]))
        ],
        axis=1,
    )
    total = tap_dot(windows, spatial_full)
    section = (latents.astype(jnp.float32) + total.reshape(latents.shape)).astype(jnp.bfloat16)
    second = group_silu(section, second_gain)
    beside_all = with_halo(second, FSDP, 1)
    frames = jnp.moveaxis(beside_all, 1, 2).reshape(-1, temporal_full.shape[0], width)
    total = tap_dot(frames, temporal_full)
    denoised = (section.astype(jnp.float32) + total.reshape(latents.shape)).astype(jnp.bfloat16)

    groups = mine[0].shape[0]
    slots = cands * CAP
    spread_x = lax.axis_size("x")
    spread_y = lax.axis_size("y")
    raw = targets.reshape(-1)
    rel_y = (raw // spread_x - lax.axis_index("y") + 2) % spread_y
    rel_x = (raw % spread_x - lax.axis_index("x") + 2) % spread_x
    flat_targets = rel_y * spread_x + rel_x
    chosen = (flat_targets[:, None] == jnp.arange(groups, dtype=jnp.int32)[None, :]).astype(
        jnp.int32
    )
    earlier = jnp.cumsum(chosen, axis=0) - chosen
    slot_of = jnp.sum(earlier * chosen, axis=1)
    live = jnp.repeat(feasible.reshape(-1), IMG_ROWS) > 0
    position = flat_targets * slots + slot_of
    placing = (
        (jnp.arange(groups * slots, dtype=jnp.int32)[:, None] == position[None, :]) & live[None, :]
    ).astype(jnp.bfloat16)
    rows = denoised.reshape(cands * IMG_ROWS, IMG_COLS, width)
    block = (
        jnp.einsum("qr,rpc->qpc", placing, rows, preferred_element_type=jnp.float32)
        .astype(jnp.bfloat16)
        .reshape(groups, slots * IMG_COLS, width)
    )

    def grads_of(packed_all):
        base = packed_all.shape[1] - HEAD_ROWS
        heads = (
            packed_all[:, base].astype(jnp.float32)
            + packed_all[:, base + 1].astype(jnp.float32)
            + packed_all[:, base + 2].astype(jnp.float32)
        )
        w = packed_all[:, :base]
        pre = jnp.einsum("gtc,gch->gth", block, w, preferred_element_type=jnp.float32)
        slope = ((1.0 - jnp.tanh(pre) ** 2) * heads[:, None, :]).astype(jnp.bfloat16)
        return jnp.einsum("gth,gch->gtc", slope, w, preferred_element_type=jnp.float32)

    grads = (grads_of(mine[0]) + grads_of(other[0])).astype(jnp.bfloat16)
    returned = grads.reshape(groups * slots, IMG_COLS, width)
    back = jnp.einsum("qr,qpc->rpc", placing, returned, preferred_element_type=jnp.float32)
    guided = (rows.astype(jnp.float32) - back).astype(jnp.bfloat16)
    return guided.reshape(latents.shape)


def solution(mesh):
    fine = Mesh(np.asarray(mesh.devices).reshape(8, 2, 4, 4), ("z", "c", "y", "x"))
    in_specs = (
        P(BATCH, FSDP, None, None),
        P(),
        P(),
        P(None, None, FSDP),
        P(None, None, FSDP),
        P(BATCH, None, None),
        P(BATCH, None),
        P(BATCH, None, None),
        P(BATCH, FSDP),
    )
    out_specs = P(BATCH, FSDP, None, None)
    return jax.shard_map(
        per_device, mesh=fine, in_specs=in_specs, out_specs=out_specs, check_vma=False
    )
```

```python
import jax
import jax.numpy as jnp
import numpy as np
from jax import lax
from jax.sharding import Mesh
from jax.sharding import PartitionSpec as P

GROUPS = 32
IMG_ROWS = 32
IMG_COLS = 32
PIX = 1024
CAP = 4
FSDP = ("z", "c")
HEAD_ROWS = 8
BATCH = ("y", "x")


def with_halo(array, axis, dim):
    size, length = (lax.axis_size(axis), array.shape[dim])
    up = [(i, (i + 1) % size) for i in range(size - 1)]
    down = [(j, i) for i, j in up]
    last = lax.slice_in_dim(array, length - 1, length, axis=dim)
    leading = lax.slice_in_dim(array, 0, 1, axis=dim)
    before = lax.ppermute(last, axis, up)
    after = lax.ppermute(leading, axis, down)
    return jnp.concatenate([before, array, after], axis=dim)


def group_silu(values, gain):
    shape = values.shape
    width = shape[-1]
    grouped = values.astype(jnp.float32).reshape(-1, shape[-2], GROUPS, width // GROUPS)
    center = jnp.mean(grouped, axis=(1, 3), keepdims=True)
    spread = jnp.mean((grouped - center) ** 2, axis=(1, 3), keepdims=True)
    normed = ((grouped - center) * lax.rsqrt(spread + 1e-05)).reshape(shape) * gain
    return jax.nn.silu(normed).astype(jnp.bfloat16)


def gather_out_major(weights):
    turned = jnp.swapaxes(weights, 1, 2)
    return lax.all_gather(turned, FSDP, axis=1, tiled=True)


def ring_gather(parts, axis):
    size = lax.axis_size(axis)
    fwd = [(i, (i + 1) % size) for i in range(size)]
    bwd = [(i, (i - 1) % size) for i in range(size)]
    out = []
    for v in parts:
        from_m1 = lax.ppermute(v, axis, fwd)
        from_p1 = lax.ppermute(v, axis, bwd)
        cut = v.shape[-1] // 2
        left = lax.ppermute(from_m1[..., :cut], axis, fwd)
        right = lax.ppermute(from_p1[..., cut:], axis, bwd)
        from_m2 = jnp.concatenate([left, right], axis=-1)
        out.append(jnp.stack([from_m2, from_m1, v, from_p1]))
    return tuple(out)


def tap_dot(windows, weights):
    return lax.dot_general(
        windows, weights, (((1, 2), (0, 2)), ((), ())), preferred_element_type=jnp.float32
    )


def nt_dot(a, b):
    return lax.dot_general(a, b, (((1,), (1,)), ((), ())), preferred_element_type=jnp.float32)


def per_device(
    latents, norm_gain, second_gain, spatial_w, temporal_w, critic_w, critic_head, targets, feasible
):
    cands = latents.shape[0]
    width = latents.shape[-1]
    hid = critic_w.shape[-1]

    core = lax.axis_index("c")
    half = hid // 2
    own_w = lax.dynamic_slice_in_dim(critic_w[0], core * half, half, axis=1)
    own_h = lax.dynamic_slice_in_dim(critic_head[0], core * half, half, axis=0)
    hi = own_h.astype(jnp.bfloat16)
    rest = own_h - hi.astype(jnp.float32)
    mid = rest.astype(jnp.bfloat16)
    lo = (rest - mid.astype(jnp.float32)).astype(jnp.bfloat16)
    pad = jnp.zeros((HEAD_ROWS - 3, half), jnp.bfloat16)
    own = (jnp.concatenate([own_w, hi[None], mid[None], lo[None], pad], axis=0),)
    cut = half // 2
    first_x = ring_gather(tuple(v[..., :cut] for v in own), "x")
    first_x = ring_gather(first_x, "y")
    first_y = ring_gather(tuple(v[..., cut:] for v in own), "y")
    first_y = ring_gather(first_y, "x")
    mine = tuple(
        jnp.concatenate([a, jnp.swapaxes(b, 0, 1)], axis=-1).reshape(-1, *a.shape[2:-1], 2 * cut)
        for a, b in zip(first_x, first_y)
    )
    other = tuple(lax.ppermute(m, "c", [(0, 1), (1, 0)]) for m in mine)

    joint = jnp.concatenate([spatial_w, temporal_w], axis=0)
    joint_full = gather_out_major(joint)
    spatial_full = joint_full[: spatial_w.shape[0]]
    temporal_full = joint_full[spatial_w.shape[0] :]

    first = group_silu(latents, norm_gain)
    padded = jnp.pad(
        first.reshape(cands, IMG_ROWS, IMG_COLS, width), ((0, 0), (1, 1), (1, 1), (0, 0))
    )
    windows = jnp.stack(
        [
            padded[:, r : r + IMG_ROWS, q : q + IMG_COLS].reshape(-1, width)
            for r, q in (divmod(offset, 3) for offset in range(spatial_full.shape[0]))
        ],
        axis=1,
    )
    total = tap_dot(windows, spatial_full)
    section = (latents.astype(jnp.float32) + total.reshape(latents.shape)).astype(jnp.bfloat16)
    second = group_silu(section, second_gain)
    beside_all = with_halo(second, FSDP, 1)
    frames = jnp.moveaxis(beside_all, 1, 2).reshape(-1, temporal_full.shape[0], width)
    total = tap_dot(frames, temporal_full)
    denoised = (section.astype(jnp.float32) + total.reshape(latents.shape)).astype(jnp.bfloat16)

    groups = mine[0].shape[0]
    slots = cands * CAP
    spread_x = lax.axis_size("x")
    spread_y = lax.axis_size("y")
    raw = targets.reshape(-1)
    rel_y = (raw // spread_x - lax.axis_index("y") + 2) % spread_y
    rel_x = (raw % spread_x - lax.axis_index("x") + 2) % spread_x
    flat_targets = rel_y * spread_x + rel_x
    chosen = (flat_targets[:, None] == jnp.arange(groups, dtype=jnp.int32)[None, :]).astype(
        jnp.int32
    )
    earlier = jnp.cumsum(chosen, axis=0) - chosen
    slot_of = jnp.sum(earlier * chosen, axis=1)
    live = jnp.repeat(feasible.reshape(-1), IMG_ROWS) > 0
    position = flat_targets * slots + slot_of
    placing = (
        (jnp.arange(groups * slots, dtype=jnp.int32)[:, None] == position[None, :]) & live[None, :]
    ).astype(jnp.bfloat16)
    rows = denoised.reshape(cands * IMG_ROWS, IMG_COLS, width)
    block = (
        jnp.einsum("qr,rpc->qpc", placing, rows, preferred_element_type=jnp.float32)
        .astype(jnp.bfloat16)
        .reshape(groups, slots * IMG_COLS, width)
    )

    def grads_of(packed_all):
        base = packed_all.shape[1] - HEAD_ROWS
        index = jnp.arange(packed_all.shape[1])
        pick = ((index >= base) & (index < base + 3)).astype(jnp.bfloat16)
        heads = jnp.einsum("r,grh->gh", pick, packed_all, preferred_element_type=jnp.float32)
        w = packed_all[:, :base]
        pre = jnp.einsum("gtc,gch->gth", block, w, preferred_element_type=jnp.float32)
        slope = ((1.0 - jnp.tanh(pre) ** 2) * heads[:, None, :]).astype(jnp.bfloat16)
        return jnp.einsum("gth,gch->gtc", slope, w, preferred_element_type=jnp.float32)

    grads = (grads_of(mine[0]) + grads_of(other[0])).astype(jnp.bfloat16)
    returned = grads.reshape(groups * slots, IMG_COLS, width)
    back = jnp.einsum("qr,qpc->rpc", placing, returned, preferred_element_type=jnp.float32)
    guided = (rows.astype(jnp.float32) - back).astype(jnp.bfloat16)
    return guided.reshape(latents.shape)


def solution(mesh):
    fine = Mesh(np.asarray(mesh.devices).reshape(8, 2, 4, 4), ("z", "c", "y", "x"))
    in_specs = (
        P(BATCH, FSDP, None, None),
        P(),
        P(),
        P(None, None, FSDP),
        P(None, None, FSDP),
        P(BATCH, None, None),
        P(BATCH, None),
        P(BATCH, None, None),
        P(BATCH, FSDP),
    )
    out_specs = P(BATCH, FSDP, None, None)
    return jax.shard_map(
        per_device, mesh=fine, in_specs=in_specs, out_specs=out_specs, check_vma=False
    )
```

```python
import jax
import jax.numpy as jnp
import numpy as np
from jax import lax
from jax.sharding import Mesh
from jax.sharding import PartitionSpec as P

GROUPS = 32
IMG_ROWS = 32
IMG_COLS = 32
PIX = 1024
CAP = 4
FSDP = ("z", "c")
HEAD_ROWS = 8
BATCH = ("y", "x")


def with_halo(array, axis, dim):
    size, length = (lax.axis_size(axis), array.shape[dim])
    up = [(i, (i + 1) % size) for i in range(size - 1)]
    down = [(j, i) for i, j in up]
    last = lax.slice_in_dim(array, length - 1, length, axis=dim)
    leading = lax.slice_in_dim(array, 0, 1, axis=dim)
    before = lax.ppermute(last, axis, up)
    after = lax.ppermute(leading, axis, down)
    return jnp.concatenate([before, array, after], axis=dim)


def group_silu(values, gain):
    shape = values.shape
    width = shape[-1]
    grouped = values.astype(jnp.float32).reshape(-1, shape[-2], GROUPS, width // GROUPS)
    center = jnp.mean(grouped, axis=(1, 3), keepdims=True)
    spread = jnp.mean((grouped - center) ** 2, axis=(1, 3), keepdims=True)
    normed = ((grouped - center) * lax.rsqrt(spread + 1e-05)).reshape(shape) * gain
    return jax.nn.silu(normed).astype(jnp.bfloat16)


def gather_out_major(weights):
    turned = jnp.swapaxes(weights, 1, 2)
    return lax.all_gather(turned, FSDP, axis=1, tiled=True)


def ring_gather(parts, axis):
    size = lax.axis_size(axis)
    fwd = [(i, (i + 1) % size) for i in range(size)]
    bwd = [(i, (i - 1) % size) for i in range(size)]
    out = []
    for v in parts:
        from_m1 = lax.ppermute(v, axis, fwd)
        from_p1 = lax.ppermute(v, axis, bwd)
        cut = v.shape[-1] // 2
        left = lax.ppermute(from_m1[..., :cut], axis, fwd)
        right = lax.ppermute(from_p1[..., cut:], axis, bwd)
        from_m2 = jnp.concatenate([left, right], axis=-1)
        out.append(jnp.stack([from_m2, from_m1, v, from_p1]))
    return tuple(out)


def tap_dot(windows, weights):
    return lax.dot_general(
        windows, weights, (((1, 2), (0, 2)), ((), ())), preferred_element_type=jnp.float32
    )


def nt_dot(a, b):
    return lax.dot_general(a, b, (((1,), (1,)), ((), ())), preferred_element_type=jnp.float32)


def per_device(
    latents, norm_gain, second_gain, spatial_w, temporal_w, critic_w, critic_head, targets, feasible
):
    cands = latents.shape[0]
    width = latents.shape[-1]
    hid = critic_w.shape[-1]

    core = lax.axis_index("c")
    half = hid // 2
    own_w = lax.dynamic_slice_in_dim(critic_w[0], core * half, half, axis=1)
    own_h = lax.dynamic_slice_in_dim(critic_head[0], core * half, half, axis=0)
    hi = own_h.astype(jnp.bfloat16)
    rest = own_h - hi.astype(jnp.float32)
    mid = rest.astype(jnp.bfloat16)
    lo = (rest - mid.astype(jnp.float32)).astype(jnp.bfloat16)
    pad = jnp.zeros((HEAD_ROWS - 3, half), jnp.bfloat16)
    own = (jnp.concatenate([own_w, hi[None], mid[None], lo[None], pad], axis=0),)
    cut = half // 2
    first_x = ring_gather(tuple(v[..., :cut] for v in own), "x")
    first_y = ring_gather(tuple(v[..., cut:] for v in own), "y")

    joint = jnp.concatenate([spatial_w, temporal_w], axis=0)
    joint_full = gather_out_major(joint)
    spatial_full = joint_full[: spatial_w.shape[0]]
    temporal_full = joint_full[spatial_w.shape[0] :]

    first = group_silu(latents, norm_gain)
    padded = jnp.pad(
        first.reshape(cands, IMG_ROWS, IMG_COLS, width), ((0, 0), (1, 1), (1, 1), (0, 0))
    )
    windows = jnp.stack(
        [
            padded[:, r : r + IMG_ROWS, q : q + IMG_COLS].reshape(-1, width)
            for r, q in (divmod(offset, 3) for offset in range(spatial_full.shape[0]))
        ],
        axis=1,
    )
    first_x, first_y, windows = lax.optimization_barrier((first_x, first_y, windows))
    first_x = ring_gather(first_x, "y")
    first_y = ring_gather(first_y, "x")
    mine = tuple(
        jnp.concatenate([a, jnp.swapaxes(b, 0, 1)], axis=-1).reshape(-1, *a.shape[2:-1], 2 * cut)
        for a, b in zip(first_x, first_y)
    )
    other = tuple(lax.ppermute(m, "c", [(0, 1), (1, 0)]) for m in mine)
    total = tap_dot(windows, spatial_full)
    section = (latents.astype(jnp.float32) + total.reshape(latents.shape)).astype(jnp.bfloat16)
    second = group_silu(section, second_gain)
    beside_all = with_halo(second, FSDP, 1)
    frames = jnp.moveaxis(beside_all, 1, 2).reshape(-1, temporal_full.shape[0], width)
    total = tap_dot(frames, temporal_full)
    denoised = (section.astype(jnp.float32) + total.reshape(latents.shape)).astype(jnp.bfloat16)

    groups = mine[0].shape[0]
    slots = cands * CAP
    spread_x = lax.axis_size("x")
    spread_y = lax.axis_size("y")
    raw = targets.reshape(-1)
    rel_y = (raw // spread_x - lax.axis_index("y") + 2) % spread_y
    rel_x = (raw % spread_x - lax.axis_index("x") + 2) % spread_x
    flat_targets = rel_y * spread_x + rel_x
    chosen = (flat_targets[:, None] == jnp.arange(groups, dtype=jnp.int32)[None, :]).astype(
        jnp.int32
    )
    earlier = jnp.cumsum(chosen, axis=0) - chosen
    slot_of = jnp.sum(earlier * chosen, axis=1)
    live = jnp.repeat(feasible.reshape(-1), IMG_ROWS) > 0
    position = flat_targets * slots + slot_of
    placing = (
        (jnp.arange(groups * slots, dtype=jnp.int32)[:, None] == position[None, :]) & live[None, :]
    ).astype(jnp.bfloat16)
    rows = denoised.reshape(cands * IMG_ROWS, IMG_COLS, width)
    block = (
        jnp.einsum("qr,rpc->qpc", placing, rows, preferred_element_type=jnp.float32)
        .astype(jnp.bfloat16)
        .reshape(groups, slots * IMG_COLS, width)
    )

    def grads_of(packed_all):
        base = packed_all.shape[1] - HEAD_ROWS
        index = jnp.arange(packed_all.shape[1])
        pick = ((index >= base) & (index < base + 3)).astype(jnp.bfloat16)
        heads = jnp.einsum("r,grh->gh", pick, packed_all, preferred_element_type=jnp.float32)
        w = packed_all[:, :base]
        pre = jnp.einsum("gtc,gch->gth", block, w, preferred_element_type=jnp.float32)
        slope = ((1.0 - jnp.tanh(pre) ** 2) * heads[:, None, :]).astype(jnp.bfloat16)
        return jnp.einsum("gth,gch->gtc", slope, w, preferred_element_type=jnp.float32)

    grads = (grads_of(mine[0]) + grads_of(other[0])).astype(jnp.bfloat16)
    returned = grads.reshape(groups * slots, IMG_COLS, width)
    back = jnp.einsum("qr,qpc->rpc", placing, returned, preferred_element_type=jnp.float32)
    guided = (rows.astype(jnp.float32) - back).astype(jnp.bfloat16)
    return guided.reshape(latents.shape)


def solution(mesh):
    fine = Mesh(np.asarray(mesh.devices).reshape(8, 2, 4, 4), ("z", "c", "y", "x"))
    in_specs = (
        P(BATCH, FSDP, None, None),
        P(),
        P(),
        P(None, None, FSDP),
        P(None, None, FSDP),
        P(BATCH, None, None),
        P(BATCH, None),
        P(BATCH, None, None),
        P(BATCH, FSDP),
    )
    out_specs = P(BATCH, FSDP, None, None)
    return jax.shard_map(
        per_device, mesh=fine, in_specs=in_specs, out_specs=out_specs, check_vma=False
    )
```

```python
import jax
import jax.numpy as jnp
import numpy as np
from jax import lax
from jax.sharding import Mesh
from jax.sharding import PartitionSpec as P

GROUPS = 32
IMG_ROWS = 32
IMG_COLS = 32
PIX = 1024
CAP = 4
FSDP = ("z", "c")
HEAD_ROWS = 8
BATCH = ("y", "x")


def with_halo(array, axis, dim):
    size, length = (lax.axis_size(axis), array.shape[dim])
    up = [(i, (i + 1) % size) for i in range(size - 1)]
    down = [(j, i) for i, j in up]
    last = lax.slice_in_dim(array, length - 1, length, axis=dim)
    leading = lax.slice_in_dim(array, 0, 1, axis=dim)
    before = lax.ppermute(last, axis, up)
    after = lax.ppermute(leading, axis, down)
    return jnp.concatenate([before, array, after], axis=dim)


def group_silu(values, gain):
    shape = values.shape
    width = shape[-1]
    grouped = values.astype(jnp.float32).reshape(-1, shape[-2], GROUPS, width // GROUPS)
    center = jnp.mean(grouped, axis=(1, 3), keepdims=True)
    spread = jnp.mean((grouped - center) ** 2, axis=(1, 3), keepdims=True)
    normed = ((grouped - center) * lax.rsqrt(spread + 1e-05)).reshape(shape) * gain
    return jax.nn.silu(normed).astype(jnp.bfloat16)


def gather_out_major(weights):
    turned = jnp.swapaxes(weights, 1, 2)
    return lax.all_gather(turned, FSDP, axis=1, tiled=True)


def ring_gather(parts, axis):
    size = lax.axis_size(axis)
    fwd = [(i, (i + 1) % size) for i in range(size)]
    bwd = [(i, (i - 1) % size) for i in range(size)]
    out = []
    for v in parts:
        from_m1 = lax.ppermute(v, axis, fwd)
        from_p1 = lax.ppermute(v, axis, bwd)
        cut = v.shape[-1] // 2
        left = lax.ppermute(from_m1[..., :cut], axis, fwd)
        right = lax.ppermute(from_p1[..., cut:], axis, bwd)
        from_m2 = jnp.concatenate([left, right], axis=-1)
        out.append(jnp.stack([from_m2, from_m1, v, from_p1]))
    return tuple(out)


def tap_dot(windows, weights):
    return lax.dot_general(
        windows, weights, (((1, 2), (0, 2)), ((), ())), preferred_element_type=jnp.float32
    )


def swap_cores(value):
    return lax.ppermute(value, "c", [(0, 1), (1, 0)])


def nt_dot(a, b):
    return lax.dot_general(a, b, (((1,), (1,)), ((), ())), preferred_element_type=jnp.float32)


def per_device(
    latents, norm_gain, second_gain, spatial_w, temporal_w, critic_w, critic_head, targets, feasible
):
    cands = latents.shape[0]
    width = latents.shape[-1]
    hid = critic_w.shape[-1]

    core = lax.axis_index("c")
    half = hid // 2
    own_w = lax.dynamic_slice_in_dim(critic_w[0], core * half, half, axis=1)
    own_h = lax.dynamic_slice_in_dim(critic_head[0], core * half, half, axis=0)
    hi = own_h.astype(jnp.bfloat16)
    rest = own_h - hi.astype(jnp.float32)
    mid = rest.astype(jnp.bfloat16)
    lo = (rest - mid.astype(jnp.float32)).astype(jnp.bfloat16)
    pad = jnp.zeros((HEAD_ROWS - 3, half), jnp.bfloat16)
    own = (jnp.concatenate([own_w, hi[None], mid[None], lo[None], pad], axis=0),)
    cut = half // 2
    first_x = ring_gather(tuple(v[..., :cut] for v in own), "x")
    first_y = ring_gather(tuple(v[..., cut:] for v in own), "y")

    joint = jnp.concatenate([spatial_w, temporal_w], axis=0)
    joint_full = gather_out_major(joint)
    spatial_full = joint_full[: spatial_w.shape[0]]
    temporal_full = joint_full[spatial_w.shape[0] :]

    first = group_silu(latents, norm_gain)
    padded = jnp.pad(
        first.reshape(cands, IMG_ROWS, IMG_COLS, width), ((0, 0), (1, 1), (1, 1), (0, 0))
    )
    windows = jnp.stack(
        [
            padded[:, r : r + IMG_ROWS, q : q + IMG_COLS].reshape(-1, width)
            for r, q in (divmod(offset, 3) for offset in range(spatial_full.shape[0]))
        ],
        axis=1,
    )
    first_x, first_y, windows = lax.optimization_barrier((first_x, first_y, windows))
    first_x = ring_gather(first_x, "y")
    first_y = ring_gather(first_y, "x")
    mine = tuple(
        jnp.concatenate([a, jnp.swapaxes(b, 0, 1)], axis=-1).reshape(-1, *a.shape[2:-1], 2 * cut)
        for a, b in zip(first_x, first_y)
    )
    other = tuple(lax.ppermute(m, "c", [(0, 1), (1, 0)]) for m in mine)
    total = tap_dot(windows, spatial_full)
    section = (latents.astype(jnp.float32) + total.reshape(latents.shape)).astype(jnp.bfloat16)
    second = group_silu(section, second_gain)
    beside_all = with_halo(second, FSDP, 1)
    frames = jnp.moveaxis(beside_all, 1, 2).reshape(-1, temporal_full.shape[0], width)
    total = tap_dot(frames, temporal_full)
    denoised = (section.astype(jnp.float32) + total.reshape(latents.shape)).astype(jnp.bfloat16)

    groups = mine[0].shape[0]
    slots = cands * CAP
    spread_x = lax.axis_size("x")
    spread_y = lax.axis_size("y")
    raw = targets.reshape(-1)
    rel_y = (raw // spread_x - lax.axis_index("y") + 2) % spread_y
    rel_x = (raw % spread_x - lax.axis_index("x") + 2) % spread_x
    flat_targets = rel_y * spread_x + rel_x
    chosen = (flat_targets[:, None] == jnp.arange(groups, dtype=jnp.int32)[None, :]).astype(
        jnp.int32
    )
    earlier = jnp.cumsum(chosen, axis=0) - chosen
    slot_of = jnp.sum(earlier * chosen, axis=1)
    live = jnp.repeat(feasible.reshape(-1), IMG_ROWS) > 0
    position = flat_targets * slots + slot_of
    placing = (
        (jnp.arange(groups * slots, dtype=jnp.int32)[:, None] == position[None, :]) & live[None, :]
    ).astype(jnp.bfloat16)
    rows = denoised.reshape(cands * IMG_ROWS, IMG_COLS, width)
    block = (
        jnp.einsum("qr,rpc->qpc", placing, rows, preferred_element_type=jnp.float32)
        .astype(jnp.bfloat16)
        .reshape(groups, slots * IMG_COLS, width)
    )

    base = mine[0].shape[1] - HEAD_ROWS
    index = jnp.arange(mine[0].shape[1])
    pick = ((index >= base) & (index < base + 3)).astype(jnp.bfloat16)
    heads_mine = jnp.einsum("r,grh->gh", pick, mine[0], preferred_element_type=jnp.float32)
    heads_other = swap_cores(heads_mine)

    def grads_of(packed_all, heads):
        w = packed_all[:, :base]
        pre = jnp.einsum("gtc,gch->gth", block, w, preferred_element_type=jnp.float32)
        slope = ((1.0 - jnp.tanh(pre) ** 2) * heads[:, None, :]).astype(jnp.bfloat16)
        return jnp.einsum("gth,gch->gtc", slope, w, preferred_element_type=jnp.float32)

    grads = (grads_of(mine[0], heads_mine) + grads_of(other[0], heads_other)).astype(jnp.bfloat16)
    returned = grads.reshape(groups * slots, IMG_COLS, width)
    back = jnp.einsum("qr,qpc->rpc", placing, returned, preferred_element_type=jnp.float32)
    guided = (rows.astype(jnp.float32) - back).astype(jnp.bfloat16)
    return guided.reshape(latents.shape)


def solution(mesh):
    fine = Mesh(np.asarray(mesh.devices).reshape(8, 2, 4, 4), ("z", "c", "y", "x"))
    in_specs = (
        P(BATCH, FSDP, None, None),
        P(),
        P(),
        P(None, None, FSDP),
        P(None, None, FSDP),
        P(BATCH, None, None),
        P(BATCH, None),
        P(BATCH, None, None),
        P(BATCH, FSDP),
    )
    out_specs = P(BATCH, FSDP, None, None)
    return jax.shard_map(
        per_device, mesh=fine, in_specs=in_specs, out_specs=out_specs, check_vma=False
    )
```

```python
import jax
import jax.numpy as jnp
import numpy as np
from jax import lax
from jax.sharding import Mesh
from jax.sharding import PartitionSpec as P

GROUPS = 32
IMG_ROWS = 32
IMG_COLS = 32
PIX = 1024
CAP = 4
FSDP = ("z", "c")
HEAD_ROWS = 8
BATCH = ("y", "x")


def with_halo(array, axis, dim):
    size, length = (lax.axis_size(axis), array.shape[dim])
    up = [(i, (i + 1) % size) for i in range(size - 1)]
    down = [(j, i) for i, j in up]
    last = lax.slice_in_dim(array, length - 1, length, axis=dim)
    leading = lax.slice_in_dim(array, 0, 1, axis=dim)
    before = lax.ppermute(last, axis, up)
    after = lax.ppermute(leading, axis, down)
    return jnp.concatenate([before, array, after], axis=dim)


def group_silu(values, gain):
    shape = values.shape
    width = shape[-1]
    grouped = values.astype(jnp.float32).reshape(-1, shape[-2], GROUPS, width // GROUPS)
    center = jnp.mean(grouped, axis=(1, 3), keepdims=True)
    spread = jnp.mean((grouped - center) ** 2, axis=(1, 3), keepdims=True)
    normed = ((grouped - center) * lax.rsqrt(spread + 1e-05)).reshape(shape) * gain
    return jax.nn.silu(normed).astype(jnp.bfloat16)


def gather_out_major(weights):
    turned = jnp.swapaxes(weights, 1, 2)
    return lax.all_gather(turned, FSDP, axis=1, tiled=True)


def ring_gather(parts, axis):
    size = lax.axis_size(axis)
    fwd = [(i, (i + 1) % size) for i in range(size)]
    bwd = [(i, (i - 1) % size) for i in range(size)]
    out = []
    for v in parts:
        from_m1 = lax.ppermute(v, axis, fwd)
        from_p1 = lax.ppermute(v, axis, bwd)
        cut = v.shape[-1] // 2
        left = lax.ppermute(from_m1[..., :cut], axis, fwd)
        right = lax.ppermute(from_p1[..., cut:], axis, bwd)
        from_m2 = jnp.concatenate([left, right], axis=-1)
        out.append(jnp.stack([from_m2, from_m1, v, from_p1]))
    return tuple(out)


def tap_dot(windows, weights):
    return lax.dot_general(
        windows, weights, (((1, 2), (0, 2)), ((), ())), preferred_element_type=jnp.float32
    )


def swap_cores(value):
    return lax.ppermute(value, "c", [(0, 1), (1, 0)])


def nt_dot(a, b):
    return lax.dot_general(a, b, (((1,), (1,)), ((), ())), preferred_element_type=jnp.float32)


def per_device(
    latents, norm_gain, second_gain, spatial_w, temporal_w, critic_w, critic_head, targets, feasible
):
    cands = latents.shape[0]
    width = latents.shape[-1]
    hid = critic_w.shape[-1]

    core = lax.axis_index("c")
    half = hid // 2
    own_w = lax.dynamic_slice_in_dim(critic_w[0], core * half, half, axis=1)
    own_h = lax.dynamic_slice_in_dim(critic_head[0], core * half, half, axis=0)
    hi = own_h.astype(jnp.bfloat16)
    rest = own_h - hi.astype(jnp.float32)
    mid = rest.astype(jnp.bfloat16)
    lo = (rest - mid.astype(jnp.float32)).astype(jnp.bfloat16)
    pad = jnp.zeros((HEAD_ROWS - 3, half), jnp.bfloat16)
    own = (jnp.concatenate([own_w, hi[None], mid[None], lo[None], pad], axis=0),)
    cut = half // 2
    first_x = ring_gather(tuple(v[..., :cut] for v in own), "x")
    first_y = ring_gather(tuple(v[..., cut:] for v in own), "y")

    joint = jnp.concatenate([spatial_w, temporal_w], axis=0)
    joint_full = gather_out_major(joint)
    spatial_full = joint_full[: spatial_w.shape[0]]
    temporal_full = joint_full[spatial_w.shape[0] :]

    first = group_silu(latents, norm_gain)
    padded = jnp.pad(
        first.reshape(cands, IMG_ROWS, IMG_COLS, width), ((0, 0), (1, 1), (1, 1), (0, 0))
    )
    windows = jnp.stack(
        [
            padded[:, r : r + IMG_ROWS, q : q + IMG_COLS].reshape(-1, width)
            for r, q in (divmod(offset, 3) for offset in range(spatial_full.shape[0]))
        ],
        axis=1,
    )
    first_x, first_y, windows = lax.optimization_barrier((first_x, first_y, windows))
    first_x = ring_gather(first_x, "y")
    first_y = ring_gather(first_y, "x")
    mine = tuple(
        jnp.concatenate([a, jnp.swapaxes(b, 0, 1)], axis=-1).reshape(-1, *a.shape[2:-1], 2 * cut)
        for a, b in zip(first_x, first_y)
    )
    other = tuple(lax.ppermute(m, "c", [(0, 1), (1, 0)]) for m in mine)
    total = tap_dot(windows, spatial_full)
    section = (latents.astype(jnp.float32) + total.reshape(latents.shape)).astype(jnp.bfloat16)
    second = group_silu(section, second_gain)
    beside_all = with_halo(second, FSDP, 1)
    frames = jnp.moveaxis(beside_all, 1, 2).reshape(-1, temporal_full.shape[0], width)
    total = tap_dot(frames, temporal_full)
    denoised = (section.astype(jnp.float32) + total.reshape(latents.shape)).astype(jnp.bfloat16)

    groups = mine[0].shape[0]
    slots = cands * CAP
    spread_x = lax.axis_size("x")
    spread_y = lax.axis_size("y")
    raw = targets.reshape(-1)
    rel_y = (raw // spread_x - lax.axis_index("y") + 2) % spread_y
    rel_x = (raw % spread_x - lax.axis_index("x") + 2) % spread_x
    flat_targets = rel_y * spread_x + rel_x
    chosen = (flat_targets[:, None] == jnp.arange(groups, dtype=jnp.int32)[None, :]).astype(
        jnp.int32
    )
    earlier = jnp.cumsum(chosen, axis=0) - chosen
    slot_of = jnp.sum(earlier * chosen, axis=1)
    live = jnp.repeat(feasible.reshape(-1), IMG_ROWS) > 0
    position = flat_targets * slots + slot_of
    placing = (
        (jnp.arange(groups * slots, dtype=jnp.int32)[:, None] == position[None, :]) & live[None, :]
    ).astype(jnp.bfloat16)
    rows = denoised.reshape(cands * IMG_ROWS, IMG_COLS, width)
    placing3 = placing.reshape(groups, slots, -1)
    block = jnp.einsum(
        "gsr,rpc->gspc", placing3, rows, preferred_element_type=jnp.float32
    ).astype(jnp.bfloat16)

    base = mine[0].shape[1] - HEAD_ROWS
    index = jnp.arange(mine[0].shape[1])
    pick = ((index >= base) & (index < base + 3)).astype(jnp.bfloat16)
    heads_mine = jnp.einsum("r,grh->gh", pick, mine[0], preferred_element_type=jnp.float32)
    heads_other = swap_cores(heads_mine)

    def grads_of(packed_all, heads):
        w = packed_all[:, :base]
        pre = jnp.einsum("gspc,gch->gsph", block, w, preferred_element_type=jnp.float32)
        slope = ((1.0 - jnp.tanh(pre) ** 2) * heads[:, None, None, :]).astype(jnp.bfloat16)
        return jnp.einsum("gsph,gch->gspc", slope, w, preferred_element_type=jnp.float32)

    grads = (grads_of(mine[0], heads_mine) + grads_of(other[0], heads_other)).astype(jnp.bfloat16)
    back = jnp.einsum("gsr,gspc->rpc", placing3, grads, preferred_element_type=jnp.float32)
    guided = (rows.astype(jnp.float32) - back).astype(jnp.bfloat16)
    return guided.reshape(latents.shape)


def solution(mesh):
    fine = Mesh(np.asarray(mesh.devices).reshape(8, 2, 4, 4), ("z", "c", "y", "x"))
    in_specs = (
        P(BATCH, FSDP, None, None),
        P(),
        P(),
        P(None, None, FSDP),
        P(None, None, FSDP),
        P(BATCH, None, None),
        P(BATCH, None),
        P(BATCH, None, None),
        P(BATCH, FSDP),
    )
    out_specs = P(BATCH, FSDP, None, None)
    return jax.shard_map(
        per_device, mesh=fine, in_specs=in_specs, out_specs=out_specs, check_vma=False
    )
```
